32 devices in a mesh: dp: 2 (over y), vocab: 16 (over z, x, core).
Axes of the slice: x: 2, y: 2, z: 4, core: 2. Of those that a mesh axis runs over, the one named last changes fastest.
Arguments:
- hidden: bfloat16 [256, 8192], P('dp', 'vocab')
- weight: bfloat16 [16384, 8192], P('vocab', 'dp')
- teacher_ids: int32 [256, 64], P('dp'), may hold values from 0 to 16383, as said below
- teacher_logp: float32 [256, 64], P('dp'), may hold values from -12 to 0
- union_blocks: int32 [2, 16], replicated, may hold values from 0 to 127, as said below
Outputs:
- loss: float32 [256], P('dp')
- grad_hidden: bfloat16 [256, 8192], P('dp', 'vocab')
- grad_weight: bfloat16 [16384, 8192], P('vocab', 'dp')
The draws below stay inside these ranges and needn't reach their ends.
Inputs may be any that keep to these rules, and one draw needn't show every extreme that they name: `union_blocks`: each row lists distinct blocks; at most 2 blocks of a row lie among the 8 blocks of one index of vocab (blocks b with b // 8 equal), and every row reaches 2 for some index. `teacher_ids`: the entries of a row are distinct and lie in blocks listed in union_blocks for the token's tile.
All inputs are finite; a program needn't handle non-finite values.
Results may differ from the reference program's by a relative error of at most 0.0053.
Values may be sent and summed in bfloat16 or wider, within the bound.
No kernel may reach another device: no remote copies, remote signals or barrier semaphores. Data moves between devices by JAX's collectives and lax.ppermute only.
A program may use at most 128 MiB of HBM per device.

```python
import math
import jax
import jax.numpy as jnp
from jax import lax

D = 8192
BLOCK = 128
VB_DEV = 8
TOPK = 64
TOK_DEV = 128
UNION = 16
TOKENS = 256
VOCAB = 16384
N_DP = 2
N_VOCAB = 16


def union_table(key):
    base = jax.random.fold_in(key, 11)
    key_a, key_b, key_c, key_d = jax.random.split(base, 4)
    first = jax.random.randint(key_a, (N_DP, N_VOCAB), 0, VB_DEV)
    second = (first + jax.random.randint(key_b, (N_DP, N_VOCAB), 1, VB_DEV)) % VB_DEV
    starts = jnp.arange(N_VOCAB, dtype=jnp.int32) * VB_DEV
    candidates = jnp.stack([starts + first, starts + second], axis=-1).reshape(N_DP, 2 * N_VOCAB)
    order = jnp.arange(2 * N_VOCAB, dtype=jnp.int32)
    scores = jax.random.randint(key_c, (N_DP, 2 * N_VOCAB), 0, 2 ** 20) * (2 * N_VOCAB) + order[None, :]
    forced = jax.random.randint(key_d, (N_DP, 1), 0, N_VOCAB)
    scores = scores + jnp.where(order[None, :] // 2 == forced, 2 ** 28, 0)
    _, picked = lax.top_k(scores, UNION)
    return jnp.take_along_axis(candidates, picked, axis=1).astype(jnp.int32)


def weight_rows(key, rows):
    base = jax.random.fold_in(key, 13)

    def one_row(index):
        return jax.random.normal(jax.random.fold_in(base, index), (D,), jnp.float32)
    return jax.vmap(one_row)(rows) * (3.0 / math.sqrt(D))


def draw_union_blocks(key, part):
    return union_table(key)


def draw_teacher_ids(key, part):
    table = union_table(key)
    span = UNION * BLOCK
    scores = jax.random.randint(jax.random.fold_in(key, 12), (TOKENS, span), 0, 2 ** 14) * span + jnp.arange(span, dtype=jnp.int32)[None, :]
    _, places = lax.top_k(scores, TOPK)
    tiles = jnp.arange(TOKENS, dtype=jnp.int32) // TOK_DEV
    chosen = jnp.take_along_axis(table[tiles], places // BLOCK, axis=1)
    return (chosen * BLOCK + places % BLOCK).astype(jnp.int32)


def draw_weight(key, part):
    return weight_rows(key, jnp.arange(VOCAB, dtype=jnp.int32)).astype(jnp.bfloat16)


def draw_hidden(key, part):
    inner = jax.random.fold_in(key, 14)
    drawn = jax.random.normal(inner, (TOKENS, D), jnp.float32)
    return drawn.astype(jnp.bfloat16)


def block_levels(rng, shape, shards, least, high):
    def one(position, blocks):
        heights = jax.random.uniform(jax.random.fold_in(jax.random.fold_in(rng, 6), position), (blocks,), jnp.float32, least / len(shards), high / len(shards))
        return jnp.repeat(jnp.exp(heights), shape[position] // blocks).reshape((-1,) + (1,) * (len(shape) - position - 1))

    level = one(*shards[0])
    for cut in shards[1:]:
        level = level * one(*cut)
    return level


def setup_inputs(seed: int = 0) -> dict:
    key_of = jax.random.split(jax.random.key(seed), 6)
    return {
        "hidden": draw_hidden(jax.random.fold_in(key_of[5], 71), 0),
        "weight": draw_weight(jax.random.fold_in(key_of[5], 71), 0),
        "teacher_ids": draw_teacher_ids(jax.random.fold_in(key_of[5], 71), 0),
        "teacher_logp": jnp.clip(-12.0 + 12.0 * jax.random.uniform(key_of[3], (TOKENS, TOPK), jnp.float32) ** block_levels(key_of[3], (TOKENS, TOPK), ((0, 2),), -0.2, 0.2), -12.0, 0.0),
        "union_blocks": draw_union_blocks(jax.random.fold_in(key_of[5], 71), 0),
    }


def reference(hidden, weight, teacher_ids, teacher_logp, union_blocks):
    nblk = weight.shape[0] // BLOCK
    blocks = weight.reshape(nblk, BLOCK, D)
    acc = jnp.zeros((nblk, BLOCK, D), jnp.float32)
    width = UNION * BLOCK
    span = jnp.arange(width, dtype=jnp.int32)
    places = jnp.arange(UNION, dtype=jnp.int32) * BLOCK
    losses = []
    grads = []
    for tile in range(N_DP):
        rows = hidden[tile * TOK_DEV:(tile + 1) * TOK_DEV]
        chosen = union_blocks[tile]
        w_union = blocks[chosen].reshape(width, D)
        logits = jnp.dot(rows, w_union.T, preferred_element_type=jnp.float32)
        ids = teacher_ids[tile * TOK_DEV:(tile + 1) * TOK_DEV]
        probs_t = jax.nn.softmax(teacher_logp[tile * TOK_DEV:(tile + 1) * TOK_DEV].astype(jnp.float32), axis=-1)
        match = (ids // BLOCK)[:, :, None] == chosen[None, None, :]
        column = jnp.sum(jnp.where(match, places[None, None, :] + (ids % BLOCK)[:, :, None], 0), axis=-1)
        onehot = (column[:, :, None] == span[None, None, :]).astype(jnp.float32)
        target = jnp.einsum("tk,tkc->tc", probs_t, onehot)
        top = jnp.max(logits, axis=1, keepdims=True)
        lse = top + jnp.log(jnp.sum(jnp.exp(logits - top), axis=1, keepdims=True))
        losses.append(lse[:, 0] - jnp.sum(target * logits, axis=1))
        dlog = (jnp.exp(logits - lse) - target).astype(jnp.bfloat16)
        grads.append(jnp.dot(dlog, w_union, preferred_element_type=jnp.float32).astype(jnp.bfloat16))
        part = jnp.dot(dlog.T, rows, preferred_element_type=jnp.float32).astype(jnp.bfloat16)
        acc = acc.at[chosen].add(part.reshape(UNION, BLOCK, D).astype(jnp.float32))
    loss = jnp.concatenate(losses, axis=0)
    grad_hidden = jnp.concatenate(grads, axis=0)
    grad_weight = acc.reshape(nblk * BLOCK, D).astype(jnp.bfloat16)
    return loss, grad_hidden, grad_weight
```

```python
import jax
import jax.numpy as jnp
from jax import lax
from jax.sharding import PartitionSpec as P

BLOCK = 128
SLOTS = 2


negative = -1e30


def slot_table(union_blocks, column, per_dev):
    inside = union_blocks // per_dev == column
    rank = jnp.cumsum(inside.astype(jnp.int32), axis=1) - 1
    slot_ids = jnp.arange(SLOTS, dtype=jnp.int32)
    picks = inside[:, :, None] & (rank[:, :, None] == slot_ids[None, None, :])
    return jnp.sum(jnp.where(picks, union_blocks[:, :, None] + 1, 0), axis=1) - 1


def shards(hidden, weight, teacher_ids, teacher_logp, union_blocks):
    tokens_here = hidden.shape[0]
    n_groups = lax.axis_size("dp")
    per_dev = weight.shape[0] // BLOCK
    piece = weight.shape[1]
    width = SLOTS * BLOCK
    dp_row = lax.axis_index("dp")
    column = lax.axis_index("vocab")
    table = slot_table(union_blocks, column, per_dev)
    filled = table >= 0
    local = jnp.where(filled, table - column * per_dev, -1)
    blocks = weight.reshape(per_dev, BLOCK, piece)
    chosen = jnp.take(blocks, jnp.maximum(local, 0).reshape(-1), axis=0).reshape(
        n_groups, width, piece
    )
    full_rows = lax.all_gather(hidden, "vocab", axis=1, tiled=True)
    wide = full_rows.reshape(tokens_here, n_groups, piece)
    own_slots = lax.dynamic_index_in_dim(table, dp_row, 0, keepdims=False)
    col_mask = jnp.repeat(own_slots >= 0, BLOCK)
    rows_w = lax.all_to_all(chosen, "dp", split_axis=0, concat_axis=0, tiled=True)
    logits = jnp.einsum("tkd,krd->tr", wide, rows_w, preferred_element_type=jnp.float32)
    offsets = teacher_ids % BLOCK
    match = (teacher_ids // BLOCK)[:, :, None] == own_slots[None, None, :]
    starts = jnp.arange(SLOTS, dtype=jnp.int32) * BLOCK
    position = jnp.sum(jnp.where(match, starts[None, None, :] + offsets[:, :, None], 0), axis=-1)
    hit = jnp.any(match, axis=-1)
    teacher_q = jax.nn.softmax(teacher_logp, axis=-1) * hit.astype(jnp.float32)
    onehot = (position[:, :, None] == jnp.arange(width, dtype=jnp.int32)[None, None, :]).astype(
        jnp.float32
    )
    target = jnp.einsum("tk,tkr->tr", teacher_q, onehot)
    masked = jnp.where(col_mask[None, :], logits, negative)
    local_top = jnp.max(masked, axis=1)
    aimed = jnp.sum(target * logits, axis=1)
    local_total = jnp.sum(jnp.where(col_mask[None, :], jnp.exp(masked - local_top[:, None]), 0.0), axis=1)
    stats = lax.all_gather(jnp.stack([local_top, local_total, aimed]), "vocab")
    top = jnp.max(stats[:, 0], axis=0)
    total = jnp.sum(stats[:, 1] * jnp.exp(stats[:, 0] - top[None, :]), axis=0)
    picked = jnp.sum(stats[:, 2], axis=0)
    lse = top + jnp.log(total)
    loss = lse - picked
    probs = jnp.where(col_mask[None, :], jnp.exp(logits - lse[:, None]), 0.0)
    dlog = (probs - target).astype(jnp.bfloat16)
    hidden_terms = jnp.einsum("tr,krd->tkd", dlog, rows_w, preferred_element_type=jnp.float32)
    pieces_w = jnp.einsum("tr,tkd->krd", dlog, wide, preferred_element_type=jnp.float32).astype(
        jnp.bfloat16
    )
    received = lax.all_to_all(pieces_w, "dp", split_axis=0, concat_axis=0, tiled=True)
    hidden_terms = hidden_terms.reshape(tokens_here, n_groups * piece)
    grad_hidden = lax.psum_scatter(hidden_terms, "vocab", scatter_dimension=1, tiled=True).astype(
        jnp.bfloat16
    )
    spread = received.reshape(n_groups * SLOTS, BLOCK, piece)
    owners = local.reshape(-1)
    block_ids = jnp.arange(per_dev, dtype=jnp.int32)[:, None, None]
    grad_weight = jnp.zeros((per_dev, BLOCK, piece), jnp.float32)
    for q in range(n_groups * SLOTS):
        grad_weight = grad_weight + jnp.where(
            block_ids == owners[q], spread[q][None].astype(jnp.float32), 0.0
        )
    grad_weight = grad_weight.astype(jnp.bfloat16).reshape(per_dev * BLOCK, piece)
    return (loss, grad_hidden, grad_weight)


def solution(mesh):
    return jax.shard_map(
        shards,
        mesh=mesh,
        in_specs=(P("dp", "vocab"), P("vocab", "dp"), P("dp", None), P("dp", None), P()),
        out_specs=(P("dp"), P("dp", "vocab"), P("vocab", "dp")),
        check_vma=False,
    )
```

```python
import jax
import jax.numpy as jnp
from jax import lax
from jax.sharding import PartitionSpec as P

BLOCK = 128
SLOTS = 2


negative = -1e30


def slot_table(union_blocks, column, per_dev):
    inside = union_blocks // per_dev == column
    rank = jnp.cumsum(inside.astype(jnp.int32), axis=1) - 1
    slot_ids = jnp.arange(SLOTS, dtype=jnp.int32)
    picks = inside[:, :, None] & (rank[:, :, None] == slot_ids[None, None, :])
    return jnp.sum(jnp.where(picks, union_blocks[:, :, None] + 1, 0), axis=1) - 1


def shards(hidden, weight, teacher_ids, teacher_logp, union_blocks):
    tokens_here = hidden.shape[0]
    n_groups = lax.axis_size("dp")
    per_dev = weight.shape[0] // BLOCK
    piece = weight.shape[1]
    width = SLOTS * BLOCK
    dp_row = lax.axis_index("dp")
    column = lax.axis_index("vocab")
    table = slot_table(union_blocks, column, per_dev)
    filled = table >= 0
    local = jnp.where(filled, table - column * per_dev, -1)
    blocks = weight.reshape(per_dev, BLOCK, piece)
    chosen = jnp.take(blocks, jnp.maximum(local, 0).reshape(-1), axis=0).reshape(
        n_groups, width, piece
    )
    full_rows = lax.all_gather(hidden, "vocab", axis=1, tiled=True)
    wide = full_rows.reshape(tokens_here, n_groups, piece)
    halves = lax.all_to_all(wide, "dp", split_axis=1, concat_axis=1, tiled=True)
    own_slots = lax.dynamic_index_in_dim(table, dp_row, 0, keepdims=False)
    col_mask = jnp.repeat(own_slots >= 0, BLOCK)
    rows_w = lax.all_to_all(chosen, "dp", split_axis=0, concat_axis=0, tiled=True)
    logits = jnp.einsum("tkd,krd->tr", wide, rows_w, preferred_element_type=jnp.float32)
    offsets = teacher_ids % BLOCK
    match = (teacher_ids // BLOCK)[:, :, None] == own_slots[None, None, :]
    starts = jnp.arange(SLOTS, dtype=jnp.int32) * BLOCK
    position = jnp.sum(jnp.where(match, starts[None, None, :] + offsets[:, :, None], 0), axis=-1)
    hit = jnp.any(match, axis=-1)
    teacher_q = jax.nn.softmax(teacher_logp, axis=-1) * hit.astype(jnp.float32)
    onehot = (position[:, :, None] == jnp.arange(width, dtype=jnp.int32)[None, None, :]).astype(
        jnp.float32
    )
    target = jnp.einsum("tk,tkr->tr", teacher_q, onehot)
    masked = jnp.where(col_mask[None, :], logits, negative)
    local_top = jnp.max(masked, axis=1)
    aimed = jnp.sum(target * logits, axis=1)
    local_total = jnp.sum(jnp.where(col_mask[None, :], jnp.exp(masked - local_top[:, None]), 0.0), axis=1)
    stats = lax.all_gather(jnp.stack([local_top, local_total, aimed]), "vocab")
    top = jnp.max(stats[:, 0], axis=0)
    total = jnp.sum(stats[:, 1] * jnp.exp(stats[:, 0] - top[None, :]), axis=0)
    picked = jnp.sum(stats[:, 2], axis=0)
    lse = top + jnp.log(total)
    loss = lse - picked
    probs = jnp.where(col_mask[None, :], jnp.exp(logits - lse[:, None]), 0.0)
    dlog = (probs - target).astype(jnp.bfloat16)
    hidden_terms = jnp.einsum("tr,krd->tkd", dlog, rows_w, preferred_element_type=jnp.float32)
    hidden_terms = hidden_terms.reshape(tokens_here, n_groups * piece)
    grad_hidden = lax.psum_scatter(hidden_terms, "vocab", scatter_dimension=1, tiled=True).astype(
        jnp.bfloat16
    )
    dlog_all = lax.all_gather(dlog, "dp").reshape(n_groups, tokens_here, SLOTS, BLOCK)
    block_ids = jnp.arange(per_dev, dtype=jnp.int32)
    placed = jnp.zeros((n_groups, tokens_here, per_dev, BLOCK), jnp.bfloat16)
    for q in range(SLOTS):
        hit_q = local[:, q][:, None] == block_ids[None, :]
        placed = placed + jnp.where(
            hit_q[:, None, :, None], dlog_all[:, :, q, :][:, :, None, :], jnp.zeros((), jnp.bfloat16)
        )
    placed = placed.reshape(n_groups, tokens_here, per_dev * BLOCK)
    grad_weight = jnp.einsum(
        "str,tsd->rd", placed, halves, preferred_element_type=jnp.float32
    ).astype(jnp.bfloat16)
    return (loss, grad_hidden, grad_weight)


def solution(mesh):
    return jax.shard_map(
        shards,
        mesh=mesh,
        in_specs=(P("dp", "vocab"), P("vocab", "dp"), P("dp", None), P("dp", None), P()),
        out_specs=(P("dp"), P("dp", "vocab"), P("vocab", "dp")),
        check_vma=False,
    )
```

```python
import jax
import jax.numpy as jnp
from jax import lax
from jax.sharding import PartitionSpec as P

BLOCK = 128
SLOTS = 2


negative = -1e30


def slot_table(union_blocks, column, per_dev):
    inside = union_blocks // per_dev == column
    rank = jnp.cumsum(inside.astype(jnp.int32), axis=1) - 1
    slot_ids = jnp.arange(SLOTS, dtype=jnp.int32)
    picks = inside[:, :, None] & (rank[:, :, None] == slot_ids[None, None, :])
    return jnp.sum(jnp.where(picks, union_blocks[:, :, None] + 1, 0), axis=1) - 1


def shards(hidden, weight, teacher_ids, teacher_logp, union_blocks):
    tokens_here = hidden.shape[0]
    n_groups = lax.axis_size("dp")
    per_dev = weight.shape[0] // BLOCK
    piece = weight.shape[1]
    width = SLOTS * BLOCK
    dp_row = lax.axis_index("dp")
    column = lax.axis_index("vocab")
    table = slot_table(union_blocks, column, per_dev)
    filled = table >= 0
    local = jnp.where(filled, table - column * per_dev, -1)
    blocks = weight.reshape(per_dev, BLOCK, piece)
    chosen = jnp.take(blocks, jnp.maximum(local, 0).reshape(-1), axis=0, mode="clip").reshape(
        n_groups, width, piece
    )
    full_rows = lax.all_gather(hidden, "vocab", axis=1, tiled=True)
    wide = full_rows.reshape(tokens_here, n_groups, piece)
    halves = lax.all_to_all(wide, "dp", split_axis=1, concat_axis=1, tiled=True)
    own_slots = lax.dynamic_index_in_dim(table, dp_row, 0, keepdims=False)
    col_mask = jnp.repeat(own_slots >= 0, BLOCK)
    rows_w = lax.all_to_all(chosen, "dp", split_axis=0, concat_axis=0, tiled=True)
    logits = jnp.einsum("tkd,krd->tr", wide, rows_w, preferred_element_type=jnp.float32)
    offsets = teacher_ids % BLOCK
    match = (teacher_ids // BLOCK)[:, :, None] == own_slots[None, None, :]
    starts = jnp.arange(SLOTS, dtype=jnp.int32) * BLOCK
    position = jnp.sum(jnp.where(match, starts[None, None, :] + offsets[:, :, None], 0), axis=-1)
    hit = jnp.any(match, axis=-1)
    teacher_q = jax.nn.softmax(teacher_logp, axis=-1) * hit.astype(jnp.float32)
    onehot = (position[:, :, None] == jnp.arange(width, dtype=jnp.int32)[None, None, :]).astype(
        jnp.float32
    )
    target = jnp.einsum("tk,tkr->tr", teacher_q, onehot)
    masked = jnp.where(col_mask[None, :], logits, negative)
    local_top = jnp.max(masked, axis=1)
    aimed = jnp.sum(target * logits, axis=1)
    local_total = jnp.sum(jnp.where(col_mask[None, :], jnp.exp(masked - local_top[:, None]), 0.0), axis=1)
    stats = lax.all_gather(jnp.stack([local_top, local_total, aimed]), "vocab")
    top = jnp.max(stats[:, 0], axis=0)
    total = jnp.sum(stats[:, 1] * jnp.exp(stats[:, 0] - top[None, :]), axis=0)
    picked = jnp.sum(stats[:, 2], axis=0)
    lse = top + jnp.log(total)
    loss = lse - picked
    probs = jnp.where(col_mask[None, :], jnp.exp(logits - lse[:, None]), 0.0)
    dlog = (probs - target).astype(jnp.bfloat16)
    hidden_terms = jnp.einsum("tr,krd->tkd", dlog, rows_w, preferred_element_type=jnp.float32)
    hidden_terms = hidden_terms.reshape(tokens_here, n_groups * piece)
    grad_hidden = lax.psum_scatter(hidden_terms, "vocab", scatter_dimension=1, tiled=True).astype(
        jnp.bfloat16
    )
    dlog_all = lax.all_gather(dlog, "dp").reshape(n_groups, tokens_here, SLOTS, BLOCK)
    block_ids = jnp.arange(per_dev, dtype=jnp.int32)
    placed = jnp.zeros((n_groups, tokens_here, per_dev, BLOCK), jnp.bfloat16)
    for q in range(SLOTS):
        hit_q = local[:, q][:, None] == block_ids[None, :]
        placed = placed + jnp.where(
            hit_q[:, None, :, None], dlog_all[:, :, q, :][:, :, None, :], jnp.zeros((), jnp.bfloat16)
        )
    placed = placed.reshape(n_groups, tokens_here, per_dev * BLOCK)
    grad_weight = jnp.einsum(
        "str,tsd->rd", placed, halves, preferred_element_type=jnp.float32
    ).astype(jnp.bfloat16)
    return (loss, grad_hidden, grad_weight)


def solution(mesh):
    return jax.shard_map(
        shards,
        mesh=mesh,
        in_specs=(P("dp", "vocab"), P("vocab", "dp"), P("dp", None), P("dp", None), P()),
        out_specs=(P("dp"), P("dp", "vocab"), P("vocab", "dp")),
        check_vma=False,
    )
```

```python
import jax
import jax.numpy as jnp
from jax import lax
from jax.sharding import PartitionSpec as P

BLOCK = 128
SLOTS = 2


negative = -1e30


def slot_table(union_blocks, column, per_dev):
    inside = union_blocks // per_dev == column
    rank = jnp.cumsum(inside.astype(jnp.int32), axis=1) - 1
    slot_ids = jnp.arange(SLOTS, dtype=jnp.int32)
    picks = inside[:, :, None] & (rank[:, :, None] == slot_ids[None, None, :])
    return jnp.sum(jnp.where(picks, union_blocks[:, :, None] + 1, 0), axis=1) - 1


def combine_stats(top, total, picked):
    n = lax.axis_size("vocab")
    if n & (n - 1):
        stats = lax.all_gather(jnp.stack([top, total, picked]), "vocab")
        best = jnp.max(stats[:, 0], axis=0)
        total = jnp.sum(stats[:, 1] * jnp.exp(stats[:, 0] - best[None, :]), axis=0)
        return best, total, jnp.sum(stats[:, 2], axis=0)
    bit = 1
    while bit < n:
        other = lax.ppermute(
            jnp.stack([top, total, picked]), "vocab", [(k, k ^ bit) for k in range(n)]
        )
        best = jnp.maximum(top, other[0])
        total = total * jnp.exp(top - best) + other[1] * jnp.exp(other[0] - best)
        picked = picked + other[2]
        top = best
        bit *= 2
    return top, total, picked


def shards(hidden, weight, teacher_ids, teacher_logp, union_blocks):
    tokens_here = hidden.shape[0]
    n_groups = lax.axis_size("dp")
    per_dev = weight.shape[0] // BLOCK
    piece = weight.shape[1]
    width = SLOTS * BLOCK
    dp_row = lax.axis_index("dp")
    column = lax.axis_index("vocab")
    table = slot_table(union_blocks, column, per_dev)
    filled = table >= 0
    local = jnp.where(filled, table - column * per_dev, -1)
    blocks = weight.reshape(per_dev, BLOCK, piece)
    chosen = jnp.take(blocks, jnp.maximum(local, 0).reshape(-1), axis=0, mode="clip").reshape(
        n_groups, width, piece
    )
    full_rows = lax.all_gather(hidden, "vocab", axis=1, tiled=True)
    wide = full_rows.reshape(tokens_here, n_groups, piece)
    halves = lax.all_to_all(wide, "dp", split_axis=1, concat_axis=1, tiled=True)
    own_slots = lax.dynamic_index_in_dim(table, dp_row, 0, keepdims=False)
    col_mask = jnp.repeat(own_slots >= 0, BLOCK)
    rows_w = lax.all_to_all(chosen, "dp", split_axis=0, concat_axis=0, tiled=True)
    logits = jnp.einsum("tkd,krd->tr", wide, rows_w, preferred_element_type=jnp.float32)
    offsets = teacher_ids % BLOCK
    match = (teacher_ids // BLOCK)[:, :, None] == own_slots[None, None, :]
    starts = jnp.arange(SLOTS, dtype=jnp.int32) * BLOCK
    position = jnp.sum(jnp.where(match, starts[None, None, :] + offsets[:, :, None], 0), axis=-1)
    hit = jnp.any(match, axis=-1)
    teacher_q = jax.nn.softmax(teacher_logp, axis=-1) * hit.astype(jnp.float32)
    onehot = (position[:, :, None] == jnp.arange(width, dtype=jnp.int32)[None, None, :]).astype(
        jnp.float32
    )
    target = jnp.einsum("tk,tkr->tr", teacher_q, onehot)
    masked = jnp.where(col_mask[None, :], logits, negative)
    local_top = jnp.max(masked, axis=1)
    aimed = jnp.sum(target * logits, axis=1)
    local_total = jnp.sum(jnp.where(col_mask[None, :], jnp.exp(masked - local_top[:, None]), 0.0), axis=1)
    top, total, picked = combine_stats(local_top, local_total, aimed)
    lse = top + jnp.log(total)
    loss = lse - picked
    probs = jnp.where(col_mask[None, :], jnp.exp(logits - lse[:, None]), 0.0)
    dlog = (probs - target).astype(jnp.bfloat16)
    hidden_terms = jnp.einsum("tr,krd->tkd", dlog, rows_w, preferred_element_type=jnp.float32)
    hidden_terms = hidden_terms.reshape(tokens_here, n_groups * piece)
    grad_hidden = lax.psum_scatter(hidden_terms, "vocab", scatter_dimension=1, tiled=True).astype(
        jnp.bfloat16
    )
    dlog_all = lax.all_gather(dlog, "dp").reshape(n_groups, tokens_here, SLOTS, BLOCK)
    block_ids = jnp.arange(per_dev, dtype=jnp.int32)
    placed = jnp.zeros((n_groups, tokens_here, per_dev, BLOCK), jnp.bfloat16)
    for q in range(SLOTS):
        hit_q = local[:, q][:, None] == block_ids[None, :]
        placed = placed + jnp.where(
            hit_q[:, None, :, None], dlog_all[:, :, q, :][:, :, None, :], jnp.zeros((), jnp.bfloat16)
        )
    placed = placed.reshape(n_groups, tokens_here, per_dev * BLOCK)
    grad_weight = jnp.einsum(
        "str,tsd->rd", placed, halves, preferred_element_type=jnp.float32
    ).astype(jnp.bfloat16)
    return (loss, grad_hidden, grad_weight)


def solution(mesh):
    return jax.shard_map(
        shards,
        mesh=mesh,
        in_specs=(P("dp", "vocab"), P("vocab", "dp"), P("dp", None), P("dp", None), P()),
        out_specs=(P("dp"), P("dp", "vocab"), P("vocab", "dp")),
        check_vma=False,
    )
```

```python
import jax
import jax.numpy as jnp
from jax import lax
from jax.sharding import PartitionSpec as P

BLOCK = 128
SLOTS = 2


negative = -1e30


def slot_table(union_blocks, column, per_dev):
    inside = union_blocks // per_dev == column
    rank = jnp.cumsum(inside.astype(jnp.int32), axis=1) - 1
    slot_ids = jnp.arange(SLOTS, dtype=jnp.int32)
    picks = inside[:, :, None] & (rank[:, :, None] == slot_ids[None, None, :])
    return jnp.sum(jnp.where(picks, union_blocks[:, :, None] + 1, 0), axis=1) - 1


def combine_stats(top, total, picked):
    n = lax.axis_size("vocab")
    if n & (n - 1):
        stats = lax.all_gather(jnp.stack([top, total, picked]), "vocab")
        best = jnp.max(stats[:, 0], axis=0)
        total = jnp.sum(stats[:, 1] * jnp.exp(stats[:, 0] - best[None, :]), axis=0)
        return best, total, jnp.sum(stats[:, 2], axis=0)
    bit = 1
    while bit < n:
        other = lax.ppermute(
            jnp.stack([top, total, picked]), "vocab", [(k, k ^ bit) for k in range(n)]
        )
        best = jnp.maximum(top, other[0])
        total = total * jnp.exp(top - best) + other[1] * jnp.exp(other[0] - best)
        picked = picked + other[2]
        top = best
        bit *= 2
    return top, total, picked


def halving_scatter(terms):
    n = lax.axis_size("vocab")
    if n & (n - 1):
        return lax.psum_scatter(terms, "vocab", scatter_dimension=1, tiled=True)
    me = lax.axis_index("vocab")
    rows, width = terms.shape
    part = terms.reshape(rows, n, width // n)
    bit = 1
    while bit < n:
        halves = part.reshape(rows, part.shape[1] // 2, 2, width // n)
        mine = (me // bit) % 2
        keep = lax.dynamic_index_in_dim(halves, mine, 2, keepdims=False)
        send = lax.dynamic_index_in_dim(halves, 1 - mine, 2, keepdims=False)
        got = lax.ppermute(send.astype(jnp.bfloat16), "vocab", [(k, k ^ bit) for k in range(n)])
        part = keep + got.astype(jnp.float32)
        bit *= 2
    return part.reshape(rows, width // n)


def shards(hidden, weight, teacher_ids, teacher_logp, union_blocks):
    tokens_here = hidden.shape[0]
    n_groups = lax.axis_size("dp")
    per_dev = weight.shape[0] // BLOCK
    piece = weight.shape[1]
    width = SLOTS * BLOCK
    dp_row = lax.axis_index("dp")
    column = lax.axis_index("vocab")
    table = slot_table(union_blocks, column, per_dev)
    filled = table >= 0
    local = jnp.where(filled, table - column * per_dev, -1)
    blocks = weight.reshape(per_dev, BLOCK, piece)
    chosen = jnp.take(blocks, jnp.maximum(local, 0).reshape(-1), axis=0, mode="clip").reshape(
        n_groups, width, piece
    )
    full_rows = lax.all_gather(hidden, "vocab", axis=1, tiled=True)
    wide = full_rows.reshape(tokens_here, n_groups, piece)
    halves = lax.all_to_all(wide, "dp", split_axis=1, concat_axis=1, tiled=True)
    own_slots = lax.dynamic_index_in_dim(table, dp_row, 0, keepdims=False)
    col_mask = jnp.repeat(own_slots >= 0, BLOCK)
    rows_w = lax.all_to_all(chosen, "dp", split_axis=0, concat_axis=0, tiled=True)
    logits = jnp.einsum("tkd,krd->tr", wide, rows_w, preferred_element_type=jnp.float32)
    offsets = teacher_ids % BLOCK
    match = (teacher_ids // BLOCK)[:, :, None] == own_slots[None, None, :]
    starts = jnp.arange(SLOTS, dtype=jnp.int32) * BLOCK
    position = jnp.sum(jnp.where(match, starts[None, None, :] + offsets[:, :, None], 0), axis=-1)
    hit = jnp.any(match, axis=-1)
    teacher_q = jax.nn.softmax(teacher_logp, axis=-1) * hit.astype(jnp.float32)
    onehot = (position[:, :, None] == jnp.arange(width, dtype=jnp.int32)[None, None, :]).astype(
        jnp.float32
    )
    target = jnp.einsum("tk,tkr->tr", teacher_q, onehot)
    masked = jnp.where(col_mask[None, :], logits, negative)
    local_top = jnp.max(masked, axis=1)
    aimed = jnp.sum(target * logits, axis=1)
    local_total = jnp.sum(jnp.where(col_mask[None, :], jnp.exp(masked - local_top[:, None]), 0.0), axis=1)
    top, total, picked = combine_stats(local_top, local_total, aimed)
    lse = top + jnp.log(total)
    loss = lse - picked
    probs = jnp.where(col_mask[None, :], jnp.exp(logits - lse[:, None]), 0.0)
    dlog = (probs - target).astype(jnp.bfloat16)
    hidden_terms = jnp.einsum("tr,krd->tkd", dlog, rows_w, preferred_element_type=jnp.float32)
    hidden_terms = hidden_terms.reshape(tokens_here, n_groups * piece)
    grad_hidden = halving_scatter(hidden_terms).astype(jnp.bfloat16)
    dlog_all = lax.all_gather(dlog, "dp").reshape(n_groups, tokens_here, SLOTS, BLOCK)
    block_ids = jnp.arange(per_dev, dtype=jnp.int32)
    placed = jnp.zeros((n_groups, tokens_here, per_dev, BLOCK), jnp.bfloat16)
    for q in range(SLOTS):
        hit_q = local[:, q][:, None] == block_ids[None, :]
        placed = placed + jnp.where(
            hit_q[:, None, :, None], dlog_all[:, :, q, :][:, :, None, :], jnp.zeros((), jnp.bfloat16)
        )
    placed = placed.reshape(n_groups, tokens_here, per_dev * BLOCK)
    grad_weight = jnp.einsum(
        "str,tsd->rd", placed, halves, preferred_element_type=jnp.float32
    ).astype(jnp.bfloat16)
    return (loss, grad_hidden, grad_weight)


def solution(mesh):
    return jax.shard_map(
        shards,
        mesh=mesh,
        in_specs=(P("dp", "vocab"), P("vocab", "dp"), P("dp", None), P("dp", None), P()),
        out_specs=(P("dp"), P("dp", "vocab"), P("vocab", "dp")),
        check_vma=False,
    )
```

```python
import jax
import jax.numpy as jnp
from jax import lax
from jax.sharding import PartitionSpec as P

BLOCK = 128
SLOTS = 2


negative = -1e30


def slot_table(union_blocks, column, per_dev):
    inside = union_blocks // per_dev == column
    rank = jnp.cumsum(inside.astype(jnp.int32), axis=1) - 1
    slot_ids = jnp.arange(SLOTS, dtype=jnp.int32)
    picks = inside[:, :, None] & (rank[:, :, None] == slot_ids[None, None, :])
    return jnp.sum(jnp.where(picks, union_blocks[:, :, None] + 1, 0), axis=1) - 1


def combine_stats(top, total, picked):
    n = lax.axis_size("vocab")
    if n & (n - 1):
        stats = lax.all_gather(jnp.stack([top, total, picked]), "vocab")
        best = jnp.max(stats[:, 0], axis=0)
        total = jnp.sum(stats[:, 1] * jnp.exp(stats[:, 0] - best[None, :]), axis=0)
        return best, total, jnp.sum(stats[:, 2], axis=0)
    bit = 1
    while bit < n:
        other = lax.ppermute(
            jnp.stack([top, total, picked]), "vocab", [(k, k ^ bit) for k in range(n)]
        )
        best = jnp.maximum(top, other[0])
        total = total * jnp.exp(top - best) + other[1] * jnp.exp(other[0] - best)
        picked = picked + other[2]
        top = best
        bit *= 2
    return top, total, picked


def halving_scatter(terms):
    n = lax.axis_size("vocab")
    if n & (n - 1):
        return lax.psum_scatter(terms, "vocab", scatter_dimension=1, tiled=True)
    me = lax.axis_index("vocab")
    rows, width = terms.shape
    part = terms.reshape(rows, n, width // n)
    bit = 1
    while bit < n:
        halves = part.reshape(rows, part.shape[1] // 2, 2, width // n)
        mine = (me // bit) % 2
        keep = lax.dynamic_index_in_dim(halves, mine, 2, keepdims=False)
        send = lax.dynamic_index_in_dim(halves, 1 - mine, 2, keepdims=False)
        got = lax.ppermute(send.astype(jnp.bfloat16), "vocab", [(k, k ^ bit) for k in range(n)])
        part = keep + got.astype(jnp.float32)
        bit *= 2
    return part.reshape(rows, width // n)


def doubling_gather(piece):
    n = lax.axis_size("dp")
    if n & (n - 1):
        return lax.all_gather(piece, "dp")
    me = lax.axis_index("dp")
    held = piece[None]
    bit = 1
    while bit < n:
        got = lax.ppermute(held, "dp", [(k, k ^ bit) for k in range(n)])
        low = (me // bit) % 2 == 0
        held = jnp.where(low, jnp.concatenate([held, got]), jnp.concatenate([got, held]))
        bit *= 2
    return held


def shards(hidden, weight, teacher_ids, teacher_logp, union_blocks):
    tokens_here = hidden.shape[0]
    n_groups = lax.axis_size("dp")
    per_dev = weight.shape[0] // BLOCK
    piece = weight.shape[1]
    width = SLOTS * BLOCK
    dp_row = lax.axis_index("dp")
    column = lax.axis_index("vocab")
    table = slot_table(union_blocks, column, per_dev)
    filled = table >= 0
    local = jnp.where(filled, table - column * per_dev, -1)
    blocks = weight.reshape(per_dev, BLOCK, piece)
    chosen = jnp.take(blocks, jnp.maximum(local, 0).reshape(-1), axis=0, mode="clip").reshape(
        n_groups, width, piece
    )
    full_rows = lax.all_gather(hidden, "vocab", axis=1, tiled=True)
    wide = full_rows.reshape(tokens_here, n_groups, piece)
    halves = lax.all_to_all(wide, "dp", split_axis=1, concat_axis=1, tiled=True)
    own_slots = lax.dynamic_index_in_dim(table, dp_row, 0, keepdims=False)
    col_mask = jnp.repeat(own_slots >= 0, BLOCK)
    rows_w = lax.all_to_all(chosen, "dp", split_axis=0, concat_axis=0, tiled=True)
    logits = jnp.einsum("tkd,krd->tr", wide, rows_w, preferred_element_type=jnp.float32)
    offsets = teacher_ids % BLOCK
    match = (teacher_ids // BLOCK)[:, :, None] == own_slots[None, None, :]
    starts = jnp.arange(SLOTS, dtype=jnp.int32) * BLOCK
    position = jnp.sum(jnp.where(match, starts[None, None, :] + offsets[:, :, None], 0), axis=-1)
    hit = jnp.any(match, axis=-1)
    teacher_q = jax.nn.softmax(teacher_logp, axis=-1) * hit.astype(jnp.float32)
    onehot = (position[:, :, None] == jnp.arange(width, dtype=jnp.int32)[None, None, :]).astype(
        jnp.float32
    )
    target = jnp.einsum("tk,tkr->tr", teacher_q, onehot)
    masked = jnp.where(col_mask[None, :], logits, negative)
    local_top = jnp.max(masked, axis=1)
    aimed = jnp.sum(target * logits, axis=1)
    local_total = jnp.sum(jnp.where(col_mask[None, :], jnp.exp(masked - local_top[:, None]), 0.0), axis=1)
    top, total, picked = combine_stats(local_top, local_total, aimed)
    lse = top + jnp.log(total)
    loss = lse - picked
    probs = jnp.where(col_mask[None, :], jnp.exp(logits - lse[:, None]), 0.0)
    dlog = (probs - target).astype(jnp.bfloat16)
    hidden_terms = jnp.einsum("tr,krd->tkd", dlog, rows_w, preferred_element_type=jnp.float32)
    hidden_terms = hidden_terms.reshape(tokens_here, n_groups * piece)
    grad_hidden = halving_scatter(hidden_terms).astype(jnp.bfloat16)
    dlog_all = doubling_gather(dlog).reshape(n_groups, tokens_here, SLOTS, BLOCK)
    block_ids = jnp.arange(per_dev, dtype=jnp.int32)
    placed = jnp.zeros((n_groups, tokens_here, per_dev, BLOCK), jnp.bfloat16)
    for q in range(SLOTS):
        hit_q = local[:, q][:, None] == block_ids[None, :]
        placed = placed + jnp.where(
            hit_q[:, None, :, None], dlog_all[:, :, q, :][:, :, None, :], jnp.zeros((), jnp.bfloat16)
        )
    placed = placed.reshape(n_groups, tokens_here, per_dev * BLOCK)
    grad_weight = jnp.einsum(
        "str,tsd->rd", placed, halves, preferred_element_type=jnp.float32
    ).astype(jnp.bfloat16)
    return (loss, grad_hidden, grad_weight)


def solution(mesh):
    return jax.shard_map(
        shards,
        mesh=mesh,
        in_specs=(P("dp", "vocab"), P("vocab", "dp"), P("dp", None), P("dp", None), P()),
        out_specs=(P("dp"), P("dp", "vocab"), P("vocab", "dp")),
        check_vma=False,
    )
```

```python
import jax
import jax.numpy as jnp
from jax import lax
from jax.sharding import PartitionSpec as P

BLOCK = 128
SLOTS = 2


negative = -1e30


def slot_table(union_blocks, column, per_dev):
    inside = union_blocks // per_dev == column
    rank = jnp.cumsum(inside.astype(jnp.int32), axis=1) - 1
    slot_ids = jnp.arange(SLOTS, dtype=jnp.int32)
    picks = inside[:, :, None] & (rank[:, :, None] == slot_ids[None, None, :])
    return jnp.sum(jnp.where(picks, union_blocks[:, :, None] + 1, 0), axis=1) - 1


def combine_stats(top, total, picked):
    n = lax.axis_size("vocab")
    if n & (n - 1):
        stats = lax.all_gather(jnp.stack([top, total, picked]), "vocab")
        best = jnp.max(stats[:, 0], axis=0)
        total = jnp.sum(stats[:, 1] * jnp.exp(stats[:, 0] - best[None, :]), axis=0)
        return best, total, jnp.sum(stats[:, 2], axis=0)
    bit = 1
    while bit < n:
        other = lax.ppermute(
            jnp.stack([top, total, picked]), "vocab", [(k, k ^ bit) for k in range(n)]
        )
        best = jnp.maximum(top, other[0])
        total = total * jnp.exp(top - best) + other[1] * jnp.exp(other[0] - best)
        picked = picked + other[2]
        top = best
        bit *= 2
    return top, total, picked


def halving_scatter(terms):
    n = lax.axis_size("vocab")
    if n & (n - 1):
        return lax.psum_scatter(terms, "vocab", scatter_dimension=1, tiled=True)
    me = lax.axis_index("vocab")
    rows, width = terms.shape
    part = terms.reshape(rows, n, width // n)
    bit = 1
    while bit < n:
        halves = part.reshape(rows, part.shape[1] // 2, 2, width // n)
        mine = (me // bit) % 2
        keep = lax.dynamic_index_in_dim(halves, mine, 2, keepdims=False)
        send = lax.dynamic_index_in_dim(halves, 1 - mine, 2, keepdims=False)
        got = lax.ppermute(send.astype(jnp.bfloat16), "vocab", [(k, k ^ bit) for k in range(n)])
        part = keep + got.astype(jnp.float32)
        bit *= 2
    return part.reshape(rows, width // n)


def doubling_gather(piece):
    n = lax.axis_size("dp")
    if n & (n - 1):
        return lax.all_gather(piece, "dp")
    me = lax.axis_index("dp")
    held = piece[None]
    bit = 1
    while bit < n:
        got = lax.ppermute(held, "dp", [(k, k ^ bit) for k in range(n)])
        low = (me // bit) % 2 == 0
        held = jnp.where(low, jnp.concatenate([held, got]), jnp.concatenate([got, held]))
        bit *= 2
    return held


def shift_exchange(wide):
    n = lax.axis_size("dp")
    me = lax.axis_index("dp")
    own = lax.dynamic_index_in_dim(wide, me, 1, keepdims=True)
    pieces = [own]
    for shift in range(1, n):
        send = lax.dynamic_index_in_dim(wide, (me + shift) % n, 1, keepdims=True)
        pieces.append(lax.ppermute(send, "dp", [(k, (k + shift) % n) for k in range(n)]))
    held = jnp.concatenate(pieces, axis=1)
    return jnp.take(held, (me - jnp.arange(n)) % n, axis=1, mode="clip")


def shards(hidden, weight, teacher_ids, teacher_logp, union_blocks):
    tokens_here = hidden.shape[0]
    n_groups = lax.axis_size("dp")
    per_dev = weight.shape[0] // BLOCK
    piece = weight.shape[1]
    width = SLOTS * BLOCK
    dp_row = lax.axis_index("dp")
    column = lax.axis_index("vocab")
    table = slot_table(union_blocks, column, per_dev)
    filled = table >= 0
    local = jnp.where(filled, table - column * per_dev, -1)
    blocks = weight.reshape(per_dev, BLOCK, piece)
    chosen = jnp.take(blocks, jnp.maximum(local, 0).reshape(-1), axis=0, mode="clip").reshape(
        n_groups, width, piece
    )
    full_rows = lax.all_gather(hidden, "vocab", axis=1, tiled=True)
    wide = full_rows.reshape(tokens_here, n_groups, piece)
    halves = shift_exchange(wide)
    own_slots = lax.dynamic_index_in_dim(table, dp_row, 0, keepdims=False)
    col_mask = jnp.repeat(own_slots >= 0, BLOCK)
    rows_w = lax.all_to_all(chosen, "dp", split_axis=0, concat_axis=0, tiled=True)
    logits = jnp.einsum("tkd,krd->tr", wide, rows_w, preferred_element_type=jnp.float32)
    offsets = teacher_ids % BLOCK
    match = (teacher_ids // BLOCK)[:, :, None] == own_slots[None, None, :]
    starts = jnp.arange(SLOTS, dtype=jnp.int32) * BLOCK
    position = jnp.sum(jnp.where(match, starts[None, None, :] + offsets[:, :, None], 0), axis=-1)
    hit = jnp.any(match, axis=-1)
    teacher_q = jax.nn.softmax(teacher_logp, axis=-1) * hit.astype(jnp.float32)
    onehot = (position[:, :, None] == jnp.arange(width, dtype=jnp.int32)[None, None, :]).astype(
        jnp.float32
    )
    target = jnp.einsum("tk,tkr->tr", teacher_q, onehot)
    masked = jnp.where(col_mask[None, :], logits, negative)
    local_top = jnp.max(masked, axis=1)
    aimed = jnp.sum(target * logits, axis=1)
    local_total = jnp.sum(jnp.where(col_mask[None, :], jnp.exp(masked - local_top[:, None]), 0.0), axis=1)
    top, total, picked = combine_stats(local_top, local_total, aimed)
    lse = top + jnp.log(total)
    loss = lse - picked
    probs = jnp.where(col_mask[None, :], jnp.exp(logits - lse[:, None]), 0.0)
    dlog = (probs - target).astype(jnp.bfloat16)
    hidden_terms = jnp.einsum("tr,krd->tkd", dlog, rows_w, preferred_element_type=jnp.float32)
    hidden_terms = hidden_terms.reshape(tokens_here, n_groups * piece)
    grad_hidden = halving_scatter(hidden_terms).astype(jnp.bfloat16)
    dlog_all = doubling_gather(dlog).reshape(n_groups, tokens_here, SLOTS, BLOCK)
    block_ids = jnp.arange(per_dev, dtype=jnp.int32)
    placed = jnp.zeros((n_groups, tokens_here, per_dev, BLOCK), jnp.bfloat16)
    for q in range(SLOTS):
        hit_q = local[:, q][:, None] == block_ids[None, :]
        placed = placed + jnp.where(
            hit_q[:, None, :, None], dlog_all[:, :, q, :][:, :, None, :], jnp.zeros((), jnp.bfloat16)
        )
    placed = placed.reshape(n_groups, tokens_here, per_dev * BLOCK)
    grad_weight = jnp.einsum(
        "str,tsd->rd", placed, halves, preferred_element_type=jnp.float32
    ).astype(jnp.bfloat16)
    return (loss, grad_hidden, grad_weight)


def solution(mesh):
    return jax.shard_map(
        shards,
        mesh=mesh,
        in_specs=(P("dp", "vocab"), P("vocab", "dp"), P("dp", None), P("dp", None), P()),
        out_specs=(P("dp"), P("dp", "vocab"), P("vocab", "dp")),
        check_vma=False,
    )
```

```python
import jax
import jax.numpy as jnp
from jax import lax
from jax.sharding import PartitionSpec as P

BLOCK = 128
SLOTS = 2


negative = -1e30


def slot_table(union_blocks, column, per_dev):
    inside = union_blocks // per_dev == column
    rank = jnp.cumsum(inside.astype(jnp.int32), axis=1) - 1
    slot_ids = jnp.arange(SLOTS, dtype=jnp.int32)
    picks = inside[:, :, None] & (rank[:, :, None] == slot_ids[None, None, :])
    return jnp.sum(jnp.where(picks, union_blocks[:, :, None] + 1, 0), axis=1) - 1


def combine_stats(top, total, picked):
    n = lax.axis_size("vocab")
    if n & (n - 1):
        stats = lax.all_gather(jnp.stack([top, total, picked]), "vocab")
        best = jnp.max(stats[:, 0], axis=0)
        total = jnp.sum(stats[:, 1] * jnp.exp(stats[:, 0] - best[None, :]), axis=0)
        return best, total, jnp.sum(stats[:, 2], axis=0)
    bit = 1
    while bit < n:
        other = lax.ppermute(
            jnp.stack([top, total, picked]), "vocab", [(k, k ^ bit) for k in range(n)]
        )
        best = jnp.maximum(top, other[0])
        total = total * jnp.exp(top - best) + other[1] * jnp.exp(other[0] - best)
        picked = picked + other[2]
        top = best
        bit *= 2
    return top, total, picked


def halving_scatter(terms):
    n = lax.axis_size("vocab")
    if n & (n - 1):
        return lax.psum_scatter(terms, "vocab", scatter_dimension=1, tiled=True)
    me = lax.axis_index("vocab")
    rows, width = terms.shape
    part = terms.reshape(rows, n, width // n)
    bit = 1
    while bit < n:
        halves = part.reshape(rows, part.shape[1] // 2, 2, width // n)
        mine = (me // bit) % 2
        keep = lax.dynamic_index_in_dim(halves, mine, 2, keepdims=False)
        send = lax.dynamic_index_in_dim(halves, 1 - mine, 2, keepdims=False)
        got = lax.ppermute(send.astype(jnp.bfloat16), "vocab", [(k, k ^ bit) for k in range(n)])
        part = keep + got.astype(jnp.float32)
        bit *= 2
    return part.reshape(rows, width // n)


def doubling_rows(block):
    n = lax.axis_size("vocab")
    if n & (n - 1):
        return lax.all_gather(block, "vocab", axis=1, tiled=True)
    me = lax.axis_index("vocab")
    rows, width = block.shape
    held = block[:, None, :]
    bit = n // 2
    while bit >= 1:
        got = lax.ppermute(held, "vocab", [(k, k ^ bit) for k in range(n)])
        clear = (me // bit) % 2 == 0
        low = jnp.where(clear, held, got)
        high = jnp.where(clear, got, held)
        held = jnp.stack([low, high], axis=2).reshape(rows, 2 * held.shape[1], width)
        bit //= 2
    return held.reshape(rows, n * width)


def doubling_gather(piece):
    n = lax.axis_size("dp")
    if n & (n - 1):
        return lax.all_gather(piece, "dp")
    me = lax.axis_index("dp")
    held = piece[None]
    bit = 1
    while bit < n:
        got = lax.ppermute(held, "dp", [(k, k ^ bit) for k in range(n)])
        low = (me // bit) % 2 == 0
        held = jnp.where(low, jnp.concatenate([held, got]), jnp.concatenate([got, held]))
        bit *= 2
    return held


def shift_exchange(wide):
    n = lax.axis_size("dp")
    me = lax.axis_index("dp")
    own = lax.dynamic_index_in_dim(wide, me, 1, keepdims=True)
    pieces = [own]
    for shift in range(1, n):
        send = lax.dynamic_index_in_dim(wide, (me + shift) % n, 1, keepdims=True)
        pieces.append(lax.ppermute(send, "dp", [(k, (k + shift) % n) for k in range(n)]))
    held = jnp.concatenate(pieces, axis=1)
    return jnp.take(held, (me - jnp.arange(n)) % n, axis=1, mode="clip")


def shards(hidden, weight, teacher_ids, teacher_logp, union_blocks):
    tokens_here = hidden.shape[0]
    n_groups = lax.axis_size("dp")
    per_dev = weight.shape[0] // BLOCK
    piece = weight.shape[1]
    width = SLOTS * BLOCK
    dp_row = lax.axis_index("dp")
    column = lax.axis_index("vocab")
    table = slot_table(union_blocks, column, per_dev)
    filled = table >= 0
    local = jnp.where(filled, table - column * per_dev, -1)
    blocks = weight.reshape(per_dev, BLOCK, piece)
    chosen = jnp.take(blocks, jnp.maximum(local, 0).reshape(-1), axis=0, mode="clip").reshape(
        n_groups, width, piece
    )
    full_rows = doubling_rows(hidden)
    wide = full_rows.reshape(tokens_here, n_groups, piece)
    halves = shift_exchange(wide)
    own_slots = lax.dynamic_index_in_dim(table, dp_row, 0, keepdims=False)
    col_mask = jnp.repeat(own_slots >= 0, BLOCK)
    rows_w = lax.all_to_all(chosen, "dp", split_axis=0, concat_axis=0, tiled=True)
    logits = jnp.einsum("tkd,krd->tr", wide, rows_w, preferred_element_type=jnp.float32)
    offsets = teacher_ids % BLOCK
    match = (teacher_ids // BLOCK)[:, :, None] == own_slots[None, None, :]
    starts = jnp.arange(SLOTS, dtype=jnp.int32) * BLOCK
    position = jnp.sum(jnp.where(match, starts[None, None, :] + offsets[:, :, None], 0), axis=-1)
    hit = jnp.any(match, axis=-1)
    teacher_q = jax.nn.softmax(teacher_logp, axis=-1) * hit.astype(jnp.float32)
    onehot = (position[:, :, None] == jnp.arange(width, dtype=jnp.int32)[None, None, :]).astype(
        jnp.float32
    )
    target = jnp.einsum("tk,tkr->tr", teacher_q, onehot)
    masked = jnp.where(col_mask[None, :], logits, negative)
    local_top = jnp.max(masked, axis=1)
    aimed = jnp.sum(target * logits, axis=1)
    local_total = jnp.sum(jnp.where(col_mask[None, :], jnp.exp(masked - local_top[:, None]), 0.0), axis=1)
    top, total, picked = combine_stats(local_top, local_total, aimed)
    lse = top + jnp.log(total)
    loss = lse - picked
    probs = jnp.where(col_mask[None, :], jnp.exp(logits - lse[:, None]), 0.0)
    dlog = (probs - target).astype(jnp.bfloat16)
    hidden_terms = jnp.einsum("tr,krd->tkd", dlog, rows_w, preferred_element_type=jnp.float32)
    hidden_terms = hidden_terms.reshape(tokens_here, n_groups * piece)
    grad_hidden = halving_scatter(hidden_terms).astype(jnp.bfloat16)
    dlog_all = doubling_gather(dlog).reshape(n_groups, tokens_here, SLOTS, BLOCK)
    block_ids = jnp.arange(per_dev, dtype=jnp.int32)
    placed = jnp.zeros((n_groups, tokens_here, per_dev, BLOCK), jnp.bfloat16)
    for q in range(SLOTS):
        hit_q = local[:, q][:, None] == block_ids[None, :]
        placed = placed + jnp.where(
            hit_q[:, None, :, None], dlog_all[:, :, q, :][:, :, None, :], jnp.zeros((), jnp.bfloat16)
        )
    placed = placed.reshape(n_groups, tokens_here, per_dev * BLOCK)
    grad_weight = jnp.einsum(
        "str,tsd->rd", placed, halves, preferred_element_type=jnp.float32
    ).astype(jnp.bfloat16)
    return (loss, grad_hidden, grad_weight)


def solution(mesh):
    return jax.shard_map(
        shards,
        mesh=mesh,
        in_specs=(P("dp", "vocab"), P("vocab", "dp"), P("dp", None), P("dp", None), P()),
        out_specs=(P("dp"), P("dp", "vocab"), P("vocab", "dp")),
        check_vma=False,
    )
```

```python
import jax
import jax.numpy as jnp
from jax import lax
from jax.sharding import PartitionSpec as P

BLOCK = 128
SLOTS = 2


negative = -1e30


def slot_table(union_blocks, column, per_dev):
    inside = union_blocks // per_dev == column
    rank = jnp.cumsum(inside.astype(jnp.int32), axis=1) - 1
    slot_ids = jnp.arange(SLOTS, dtype=jnp.int32)
    picks = inside[:, :, None] & (rank[:, :, None] == slot_ids[None, None, :])
    return jnp.sum(jnp.where(picks, union_blocks[:, :, None] + 1, 0), axis=1) - 1


def combine_stats(top, total, picked):
    n = lax.axis_size("vocab")
    if n & (n - 1):
        stats = lax.all_gather(jnp.stack([top, total, picked]), "vocab")
        best = jnp.max(stats[:, 0], axis=0)
        total = jnp.sum(stats[:, 1] * jnp.exp(stats[:, 0] - best[None, :]), axis=0)
        return best, total, jnp.sum(stats[:, 2], axis=0)
    bit = 1
    while bit < n:
        other = lax.ppermute(
            jnp.stack([top, total, picked]), "vocab", [(k, k ^ bit) for k in range(n)]
        )
        best = jnp.maximum(top, other[0])
        total = total * jnp.exp(top - best) + other[1] * jnp.exp(other[0] - best)
        picked = picked + other[2]
        top = best
        bit *= 2
    return top, total, picked


def halving_scatter(terms):
    n = lax.axis_size("vocab")
    if n & (n - 1):
        return lax.psum_scatter(terms, "vocab", scatter_dimension=1, tiled=True)
    me = lax.axis_index("vocab")
    rows, width = terms.shape
    part = terms.reshape(rows, n, width // n)
    bit = 1
    while bit < n:
        halves = part.reshape(rows, part.shape[1] // 2, 2, width // n)
        mine = (me // bit) % 2
        keep = lax.dynamic_index_in_dim(halves, mine, 2, keepdims=False)
        send = lax.dynamic_index_in_dim(halves, 1 - mine, 2, keepdims=False)
        got = lax.ppermute(send.astype(jnp.bfloat16), "vocab", [(k, k ^ bit) for k in range(n)])
        part = keep + got.astype(jnp.float32)
        bit *= 2
    return part.reshape(rows, width // n)


def doubling_rows(block):
    n = lax.axis_size("vocab")
    if n & (n - 1):
        return lax.all_gather(block, "vocab", axis=1, tiled=True)
    me = lax.axis_index("vocab")
    rows, width = block.shape
    held = block[:, None, :]
    bit = n // 2
    while bit >= 1:
        got = lax.ppermute(held, "vocab", [(k, k ^ bit) for k in range(n)])
        clear = (me // bit) % 2 == 0
        low = jnp.where(clear, held, got)
        high = jnp.where(clear, got, held)
        held = jnp.stack([low, high], axis=2).reshape(rows, 2 * held.shape[1], width)
        bit //= 2
    return held.reshape(rows, n * width)


def doubling_gather(piece):
    n = lax.axis_size("dp")
    if n & (n - 1):
        return lax.all_gather(piece, "dp")
    me = lax.axis_index("dp")
    held = piece[None]
    bit = 1
    while bit < n:
        got = lax.ppermute(held, "dp", [(k, k ^ bit) for k in range(n)])
        low = (me // bit) % 2 == 0
        held = jnp.where(low, jnp.concatenate([held, got]), jnp.concatenate([got, held]))
        bit *= 2
    return held


def shift_exchange(wide, axis):
    n = lax.axis_size("dp")
    me = lax.axis_index("dp")
    own = lax.dynamic_index_in_dim(wide, me, axis, keepdims=True)
    pieces = [own]
    for shift in range(1, n):
        send = lax.dynamic_index_in_dim(wide, (me + shift) % n, axis, keepdims=True)
        pieces.append(lax.ppermute(send, "dp", [(k, (k + shift) % n) for k in range(n)]))
    held = jnp.concatenate(pieces, axis=axis)
    return jnp.take(held, (me - jnp.arange(n)) % n, axis=axis, mode="clip")


def shards(hidden, weight, teacher_ids, teacher_logp, union_blocks):
    tokens_here = hidden.shape[0]
    n_groups = lax.axis_size("dp")
    per_dev = weight.shape[0] // BLOCK
    piece = weight.shape[1]
    width = SLOTS * BLOCK
    dp_row = lax.axis_index("dp")
    column = lax.axis_index("vocab")
    table = slot_table(union_blocks, column, per_dev)
    filled = table >= 0
    local = jnp.where(filled, table - column * per_dev, -1)
    blocks = weight.reshape(per_dev, BLOCK, piece)
    chosen = jnp.take(blocks, jnp.maximum(local, 0).reshape(-1), axis=0, mode="clip").reshape(
        n_groups, width, piece
    )
    full_rows = doubling_rows(hidden)
    wide = full_rows.reshape(tokens_here, n_groups, piece)
    halves = shift_exchange(wide, 1)
    own_slots = lax.dynamic_index_in_dim(table, dp_row, 0, keepdims=False)
    col_mask = jnp.repeat(own_slots >= 0, BLOCK)
    rows_w = shift_exchange(chosen, 0)
    logits = jnp.einsum("tkd,krd->tr", wide, rows_w, preferred_element_type=jnp.float32)
    offsets = teacher_ids % BLOCK
    match = (teacher_ids // BLOCK)[:, :, None] == own_slots[None, None, :]
    starts = jnp.arange(SLOTS, dtype=jnp.int32) * BLOCK
    position = jnp.sum(jnp.where(match, starts[None, None, :] + offsets[:, :, None], 0), axis=-1)
    hit = jnp.any(match, axis=-1)
    teacher_q = jax.nn.softmax(teacher_logp, axis=-1) * hit.astype(jnp.float32)
    onehot = (position[:, :, None] == jnp.arange(width, dtype=jnp.int32)[None, None, :]).astype(
        jnp.float32
    )
    target = jnp.einsum("tk,tkr->tr", teacher_q, onehot)
    masked = jnp.where(col_mask[None, :], logits, negative)
    local_top = jnp.max(masked, axis=1)
    aimed = jnp.sum(target * logits, axis=1)
    local_total = jnp.sum(jnp.where(col_mask[None, :], jnp.exp(masked - local_top[:, None]), 0.0), axis=1)
    top, total, picked = combine_stats(local_top, local_total, aimed)
    lse = top + jnp.log(total)
    loss = lse - picked
    probs = jnp.where(col_mask[None, :], jnp.exp(logits - lse[:, None]), 0.0)
    dlog = (probs - target).astype(jnp.bfloat16)
    hidden_terms = jnp.einsum("tr,krd->tkd", dlog, rows_w, preferred_element_type=jnp.float32)
    hidden_terms = hidden_terms.reshape(tokens_here, n_groups * piece)
    grad_hidden = halving_scatter(hidden_terms).astype(jnp.bfloat16)
    dlog_all = doubling_gather(dlog).reshape(n_groups, tokens_here, SLOTS, BLOCK)
    block_ids = jnp.arange(per_dev, dtype=jnp.int32)
    placed = jnp.zeros((n_groups, tokens_here, per_dev, BLOCK), jnp.bfloat16)
    for q in range(SLOTS):
        hit_q = local[:, q][:, None] == block_ids[None, :]
        placed = placed + jnp.where(
            hit_q[:, None, :, None], dlog_all[:, :, q, :][:, :, None, :], jnp.zeros((), jnp.bfloat16)
        )
    placed = placed.reshape(n_groups, tokens_here, per_dev * BLOCK)
    grad_weight = jnp.einsum(
        "str,tsd->rd", placed, halves, preferred_element_type=jnp.float32
    ).astype(jnp.bfloat16)
    return (loss, grad_hidden, grad_weight)


def solution(mesh):
    return jax.shard_map(
        shards,
        mesh=mesh,
        in_specs=(P("dp", "vocab"), P("vocab", "dp"), P("dp", None), P("dp", None), P()),
        out_specs=(P("dp"), P("dp", "vocab"), P("vocab", "dp")),
        check_vma=False,
    )
```

```python
import jax
import jax.numpy as jnp
from jax import lax
from jax.sharding import PartitionSpec as P

BLOCK = 128
SLOTS = 2


negative = -1e30


def slot_table(union_blocks, column, per_dev):
    inside = union_blocks // per_dev == column
    rank = jnp.cumsum(inside.astype(jnp.int32), axis=1) - 1
    slot_ids = jnp.arange(SLOTS, dtype=jnp.int32)
    picks = inside[:, :, None] & (rank[:, :, None] == slot_ids[None, None, :])
    return jnp.sum(jnp.where(picks, union_blocks[:, :, None] + 1, 0), axis=1) - 1


def combine_stats(top, total, picked):
    n = lax.axis_size("vocab")
    if n & (n - 1):
        stats = lax.all_gather(jnp.stack([top, total, picked]), "vocab")
        best = jnp.max(stats[:, 0], axis=0)
        total = jnp.sum(stats[:, 1] * jnp.exp(stats[:, 0] - best[None, :]), axis=0)
        return best, total, jnp.sum(stats[:, 2], axis=0)
    bit = 1
    while bit < n:
        other = lax.ppermute(
            jnp.stack([top, total, picked]), "vocab", [(k, k ^ bit) for k in range(n)]
        )
        best = jnp.maximum(top, other[0])
        total = total * jnp.exp(top - best) + other[1] * jnp.exp(other[0] - best)
        picked = picked + other[2]
        top = best
        bit *= 2
    return top, total, picked


def halving_scatter(terms, flip=0):
    n = lax.axis_size("vocab")
    if n & (n - 1):
        return lax.psum_scatter(terms, "vocab", scatter_dimension=1, tiled=True)
    me = lax.axis_index("vocab") ^ flip
    rows, width = terms.shape
    part = terms.reshape(rows, n, width // n)
    bit = 1
    while bit < n:
        halves = part.reshape(rows, part.shape[1] // 2, 2, width // n)
        mine = (me // bit) % 2
        keep = lax.dynamic_index_in_dim(halves, mine, 2, keepdims=False)
        send = lax.dynamic_index_in_dim(halves, 1 - mine, 2, keepdims=False)
        got = lax.ppermute(send.astype(jnp.bfloat16), "vocab", [(k, k ^ bit) for k in range(n)])
        part = keep + got.astype(jnp.float32)
        bit *= 2
    return part.reshape(rows, width // n)


def doubling_rows(block):
    n = lax.axis_size("vocab")
    if n & (n - 1):
        return lax.all_gather(block, "vocab", axis=1, tiled=True)
    me = lax.axis_index("vocab")
    rows, width = block.shape
    held = block[:, None, :]
    bit = n // 2
    while bit >= 1:
        got = lax.ppermute(held, "vocab", [(k, k ^ bit) for k in range(n)])
        clear = (me // bit) % 2 == 0
        low = jnp.where(clear, held, got)
        high = jnp.where(clear, got, held)
        held = jnp.stack([low, high], axis=2).reshape(rows, 2 * held.shape[1], width)
        bit //= 2
    return held.reshape(rows, n * width)


def doubling_gather(piece):
    n = lax.axis_size("dp")
    if n & (n - 1):
        return lax.all_gather(piece, "dp")
    me = lax.axis_index("dp")
    held = piece[None]
    bit = 1
    while bit < n:
        got = lax.ppermute(held, "dp", [(k, k ^ bit) for k in range(n)])
        low = (me // bit) % 2 == 0
        held = jnp.where(low, jnp.concatenate([held, got]), jnp.concatenate([got, held]))
        bit *= 2
    return held


def shift_exchange(wide, axis):
    n = lax.axis_size("dp")
    me = lax.axis_index("dp")
    own = lax.dynamic_index_in_dim(wide, me, axis, keepdims=True)
    pieces = [own]
    for shift in range(1, n):
        send = lax.dynamic_index_in_dim(wide, (me + shift) % n, axis, keepdims=True)
        pieces.append(lax.ppermute(send, "dp", [(k, (k + shift) % n) for k in range(n)]))
    held = jnp.concatenate(pieces, axis=axis)
    return jnp.take(held, (me - jnp.arange(n)) % n, axis=axis, mode="clip")


def shards(hidden, weight, teacher_ids, teacher_logp, union_blocks):
    tokens_here = hidden.shape[0]
    n_groups = lax.axis_size("dp")
    per_dev = weight.shape[0] // BLOCK
    piece = weight.shape[1]
    width = SLOTS * BLOCK
    dp_row = lax.axis_index("dp")
    column = lax.axis_index("vocab")
    table = slot_table(union_blocks, column, per_dev)
    filled = table >= 0
    local = jnp.where(filled, table - column * per_dev, -1)
    blocks = weight.reshape(per_dev, BLOCK, piece)
    chosen = jnp.take(blocks, jnp.maximum(local, 0).reshape(-1), axis=0, mode="clip").reshape(
        n_groups, width, piece
    )
    full_rows = doubling_rows(hidden)
    wide = full_rows.reshape(tokens_here, n_groups, piece)
    n_vocab = lax.axis_size("vocab")
    pair = n_groups == 2 and n_vocab % 2 == 0 and not n_vocab & (n_vocab - 1)
    if pair:
        own_half = lax.dynamic_index_in_dim(wide, dp_row, 1, keepdims=False)
        other_half = lax.dynamic_index_in_dim(wide, 1 - dp_row, 1, keepdims=False)
        got_half = lax.ppermute(other_half, "dp", [(0, 1), (1, 0)])
    else:
        halves = shift_exchange(wide, 1)
    own_slots = lax.dynamic_index_in_dim(table, dp_row, 0, keepdims=False)
    col_mask = jnp.repeat(own_slots >= 0, BLOCK)
    if pair:
        own_w = lax.dynamic_index_in_dim(chosen, dp_row, 0, keepdims=False)
        got_w = lax.ppermute(
            lax.dynamic_index_in_dim(chosen, 1 - dp_row, 0, keepdims=False),
            "dp",
            [(0, 1), (1, 0)],
        )
        held_w = jnp.stack([own_w, got_w])
    else:
        rows_w = shift_exchange(chosen, 0)
    if pair:
        logits = jnp.einsum(
            "td,rd->tr", own_half, own_w, preferred_element_type=jnp.float32
        ) + jnp.einsum("td,rd->tr", other_half, got_w, preferred_element_type=jnp.float32)
    else:
        logits = jnp.einsum("tkd,krd->tr", wide, rows_w, preferred_element_type=jnp.float32)
    offsets = teacher_ids % BLOCK
    match = (teacher_ids // BLOCK)[:, :, None] == own_slots[None, None, :]
    starts = jnp.arange(SLOTS, dtype=jnp.int32) * BLOCK
    position = jnp.sum(jnp.where(match, starts[None, None, :] + offsets[:, :, None], 0), axis=-1)
    hit = jnp.any(match, axis=-1)
    teacher_q = jax.nn.softmax(teacher_logp, axis=-1) * hit.astype(jnp.float32)
    onehot = (position[:, :, None] == jnp.arange(width, dtype=jnp.int32)[None, None, :]).astype(
        jnp.float32
    )
    target = jnp.einsum("tk,tkr->tr", teacher_q, onehot)
    masked = jnp.where(col_mask[None, :], logits, negative)
    local_top = jnp.max(masked, axis=1)
    aimed = jnp.sum(target * logits, axis=1)
    local_total = jnp.sum(jnp.where(col_mask[None, :], jnp.exp(masked - local_top[:, None]), 0.0), axis=1)
    top, total, picked = combine_stats(local_top, local_total, aimed)
    lse = top + jnp.log(total)
    loss = lse - picked
    probs = jnp.where(col_mask[None, :], jnp.exp(logits - lse[:, None]), 0.0)
    dlog = (probs - target).astype(jnp.bfloat16)
    if pair:
        hidden_terms = jnp.einsum("tr,krd->tkd", dlog, held_w, preferred_element_type=jnp.float32)
        flip = dp_row * (lax.axis_size("vocab") // 2)
    else:
        hidden_terms = jnp.einsum("tr,krd->tkd", dlog, rows_w, preferred_element_type=jnp.float32)
        flip = 0
    hidden_terms = hidden_terms.reshape(tokens_here, n_groups * piece)
    grad_hidden = halving_scatter(hidden_terms, flip).astype(jnp.bfloat16)
    dlog_all = doubling_gather(dlog).reshape(n_groups, tokens_here, SLOTS, BLOCK)
    block_ids = jnp.arange(per_dev, dtype=jnp.int32)
    placed = jnp.zeros((n_groups, tokens_here, per_dev, BLOCK), jnp.bfloat16)
    for q in range(SLOTS):
        hit_q = local[:, q][:, None] == block_ids[None, :]
        placed = placed + jnp.where(
            hit_q[:, None, :, None], dlog_all[:, :, q, :][:, :, None, :], jnp.zeros((), jnp.bfloat16)
        )
    placed = placed.reshape(n_groups, tokens_here, per_dev * BLOCK)
    if pair:
        mine_p = lax.dynamic_index_in_dim(placed, dp_row, 0, keepdims=False)
        other_p = lax.dynamic_index_in_dim(placed, 1 - dp_row, 0, keepdims=False)
        grad_weight = (
            jnp.einsum("tr,td->rd", mine_p, own_half, preferred_element_type=jnp.float32)
            + jnp.einsum("tr,td->rd", other_p, got_half, preferred_element_type=jnp.float32)
        ).astype(jnp.bfloat16)
    else:
        grad_weight = jnp.einsum(
            "str,tsd->rd", placed, halves, preferred_element_type=jnp.float32
        ).astype(jnp.bfloat16)
    return (loss, grad_hidden, grad_weight)


def solution(mesh):
    return jax.shard_map(
        shards,
        mesh=mesh,
        in_specs=(P("dp", "vocab"), P("vocab", "dp"), P("dp", None), P("dp", None), P()),
        out_specs=(P("dp"), P("dp", "vocab"), P("vocab", "dp")),
        check_vma=False,
    )
```

```python
import jax
import jax.numpy as jnp
from jax import lax
from jax.sharding import PartitionSpec as P

BLOCK = 128
SLOTS = 2


negative = -1e30


def slot_table(union_blocks, column, per_dev):
    inside = union_blocks // per_dev == column
    rank = jnp.cumsum(inside.astype(jnp.int32), axis=1) - 1
    slot_ids = jnp.arange(SLOTS, dtype=jnp.int32)
    picks = inside[:, :, None] & (rank[:, :, None] == slot_ids[None, None, :])
    return jnp.sum(jnp.where(picks, union_blocks[:, :, None] + 1, 0), axis=1) - 1


def combine_stats(top, total, picked):
    n = lax.axis_size("vocab")
    if n & (n - 1):
        stats = lax.all_gather(jnp.stack([top, total, picked]), "vocab")
        best = jnp.max(stats[:, 0], axis=0)
        total = jnp.sum(stats[:, 1] * jnp.exp(stats[:, 0] - best[None, :]), axis=0)
        return best, total, jnp.sum(stats[:, 2], axis=0)
    bit = 1
    while bit < n:
        other = lax.ppermute(
            jnp.stack([top, total, picked]), "vocab", [(k, k ^ bit) for k in range(n)]
        )
        best = jnp.maximum(top, other[0])
        total = total * jnp.exp(top - best) + other[1] * jnp.exp(other[0] - best)
        picked = picked + other[2]
        top = best
        bit *= 2
    return top, total, picked


def halving_scatter(terms, flip=0):
    n = lax.axis_size("vocab")
    if n & (n - 1):
        return lax.psum_scatter(terms, "vocab", scatter_dimension=1, tiled=True)
    me = lax.axis_index("vocab") ^ flip
    rows, width = terms.shape
    part = terms.reshape(rows, n, width // n)
    bit = 1
    while bit < n:
        halves = part.reshape(rows, part.shape[1] // 2, 2, width // n)
        mine = (me // bit) % 2
        keep = lax.dynamic_index_in_dim(halves, mine, 2, keepdims=False)
        send = lax.dynamic_index_in_dim(halves, 1 - mine, 2, keepdims=False)
        got = lax.ppermute(send.astype(jnp.bfloat16), "vocab", [(k, k ^ bit) for k in range(n)])
        part = keep + got.astype(jnp.float32)
        bit *= 2
    return part.reshape(rows, width // n)


def doubling_rows(block):
    n = lax.axis_size("vocab")
    if n & (n - 1):
        return lax.all_gather(block, "vocab", axis=1, tiled=True)
    me = lax.axis_index("vocab")
    rows, width = block.shape
    held = block[:, None, :]
    bit = n // 2
    while bit >= 1:
        got = lax.ppermute(held, "vocab", [(k, k ^ bit) for k in range(n)])
        clear = (me // bit) % 2 == 0
        low = jnp.where(clear, held, got)
        high = jnp.where(clear, got, held)
        held = jnp.stack([low, high], axis=2).reshape(rows, 2 * held.shape[1], width)
        bit //= 2
    return held.reshape(rows, n * width)


def doubling_gather(piece):
    n = lax.axis_size("dp")
    if n & (n - 1):
        return lax.all_gather(piece, "dp")
    me = lax.axis_index("dp")
    held = piece[None]
    bit = 1
    while bit < n:
        got = lax.ppermute(held, "dp", [(k, k ^ bit) for k in range(n)])
        low = (me // bit) % 2 == 0
        held = jnp.where(low, jnp.concatenate([held, got]), jnp.concatenate([got, held]))
        bit *= 2
    return held


def shift_exchange(wide, axis):
    n = lax.axis_size("dp")
    me = lax.axis_index("dp")
    own = lax.dynamic_index_in_dim(wide, me, axis, keepdims=True)
    pieces = [own]
    for shift in range(1, n):
        send = lax.dynamic_index_in_dim(wide, (me + shift) % n, axis, keepdims=True)
        pieces.append(lax.ppermute(send, "dp", [(k, (k + shift) % n) for k in range(n)]))
    held = jnp.concatenate(pieces, axis=axis)
    return jnp.take(held, (me - jnp.arange(n)) % n, axis=axis, mode="clip")


def shards(hidden, weight, teacher_ids, teacher_logp, union_blocks):
    tokens_here = hidden.shape[0]
    n_groups = lax.axis_size("dp")
    per_dev = weight.shape[0] // BLOCK
    piece = weight.shape[1]
    width = SLOTS * BLOCK
    dp_row = lax.axis_index("dp")
    column = lax.axis_index("vocab")
    table = slot_table(union_blocks, column, per_dev)
    filled = table >= 0
    local = jnp.where(filled, table - column * per_dev, -1)
    blocks = weight.reshape(per_dev, BLOCK, piece)
    chosen = jnp.take(blocks, jnp.maximum(local, 0).reshape(-1), axis=0, mode="clip").reshape(
        n_groups, width, piece
    )
    full_rows = doubling_rows(hidden)
    wide = full_rows.reshape(tokens_here, n_groups, piece)
    n_vocab = lax.axis_size("vocab")
    pair = n_groups == 2 and n_vocab % 2 == 0 and not n_vocab & (n_vocab - 1)
    if pair:
        own_half = lax.dynamic_index_in_dim(wide, dp_row, 1, keepdims=False)
        other_half = lax.dynamic_index_in_dim(wide, 1 - dp_row, 1, keepdims=False)
        got_half = lax.ppermute(other_half, "dp", [(0, 1), (1, 0)])
    else:
        halves = shift_exchange(wide, 1)
    own_slots = lax.dynamic_index_in_dim(table, dp_row, 0, keepdims=False)
    col_mask = jnp.repeat(own_slots >= 0, BLOCK)
    if pair:
        slot_rows = jnp.maximum(local, 0)

        def rows_of(tile):
            picks = lax.dynamic_index_in_dim(slot_rows, tile, 0, keepdims=False)
            return jnp.take(blocks, picks, axis=0, mode="clip").reshape(width, piece)

        got_w = lax.ppermute(rows_of(1 - dp_row), "dp", [(0, 1), (1, 0)])
        own_w = rows_of(dp_row)
        held_w = jnp.stack([own_w, got_w])
    else:
        rows_w = shift_exchange(chosen, 0)
    if pair:
        logits = jnp.einsum(
            "td,rd->tr", own_half, own_w, preferred_element_type=jnp.float32
        ) + jnp.einsum("td,rd->tr", other_half, got_w, preferred_element_type=jnp.float32)
    else:
        logits = jnp.einsum("tkd,krd->tr", wide, rows_w, preferred_element_type=jnp.float32)
    offsets = teacher_ids % BLOCK
    match = (teacher_ids // BLOCK)[:, :, None] == own_slots[None, None, :]
    starts = jnp.arange(SLOTS, dtype=jnp.int32) * BLOCK
    position = jnp.sum(jnp.where(match, starts[None, None, :] + offsets[:, :, None], 0), axis=-1)
    hit = jnp.any(match, axis=-1)
    teacher_q = jax.nn.softmax(teacher_logp, axis=-1) * hit.astype(jnp.float32)
    onehot = (position[:, :, None] == jnp.arange(width, dtype=jnp.int32)[None, None, :]).astype(
        jnp.float32
    )
    target = jnp.einsum("tk,tkr->tr", teacher_q, onehot)
    masked = jnp.where(col_mask[None, :], logits, negative)
    local_top = jnp.max(masked, axis=1)
    aimed = jnp.sum(target * logits, axis=1)
    local_total = jnp.sum(jnp.where(col_mask[None, :], jnp.exp(masked - local_top[:, None]), 0.0), axis=1)
    top, total, picked = combine_stats(local_top, local_total, aimed)
    lse = top + jnp.log(total)
    loss = lse - picked
    probs = jnp.where(col_mask[None, :], jnp.exp(logits - lse[:, None]), 0.0)
    dlog = (probs - target).astype(jnp.bfloat16)
    if pair:
        hidden_terms = jnp.einsum("tr,krd->tkd", dlog, held_w, preferred_element_type=jnp.float32)
        flip = dp_row * (lax.axis_size("vocab") // 2)
    else:
        hidden_terms = jnp.einsum("tr,krd->tkd", dlog, rows_w, preferred_element_type=jnp.float32)
        flip = 0
    hidden_terms = hidden_terms.reshape(tokens_here, n_groups * piece)
    grad_hidden = halving_scatter(hidden_terms, flip).astype(jnp.bfloat16)
    dlog_all = doubling_gather(dlog).reshape(n_groups, tokens_here, SLOTS, BLOCK)
    block_ids = jnp.arange(per_dev, dtype=jnp.int32)
    placed = jnp.zeros((n_groups, tokens_here, per_dev, BLOCK), jnp.bfloat16)
    for q in range(SLOTS):
        hit_q = local[:, q][:, None] == block_ids[None, :]
        placed = placed + jnp.where(
            hit_q[:, None, :, None], dlog_all[:, :, q, :][:, :, None, :], jnp.zeros((), jnp.bfloat16)
        )
    placed = placed.reshape(n_groups, tokens_here, per_dev * BLOCK)
    if pair:
        mine_p = lax.dynamic_index_in_dim(placed, dp_row, 0, keepdims=False)
        other_p = lax.dynamic_index_in_dim(placed, 1 - dp_row, 0, keepdims=False)
        grad_weight = jnp.einsum(
            "tr,td->rd",
            jnp.concatenate([mine_p, other_p]),
            jnp.concatenate([own_half, got_half]),
            preferred_element_type=jnp.float32,
        ).astype(jnp.bfloat16)
    else:
        grad_weight = jnp.einsum(
            "str,tsd->rd", placed, halves, preferred_element_type=jnp.float32
        ).astype(jnp.bfloat16)
    return (loss, grad_hidden, grad_weight)


def solution(mesh):
    return jax.shard_map(
        shards,
        mesh=mesh,
        in_specs=(P("dp", "vocab"), P("vocab", "dp"), P("dp", None), P("dp", None), P()),
        out_specs=(P("dp"), P("dp", "vocab"), P("vocab", "dp")),
        check_vma=False,
    )
```

```python
import jax
import jax.numpy as jnp
from jax import lax
from jax.sharding import PartitionSpec as P

BLOCK = 128
SLOTS = 2


negative = -1e30


def slot_table(union_blocks, column, per_dev):
    inside = union_blocks // per_dev == column
    rank = jnp.cumsum(inside.astype(jnp.int32), axis=1) - 1
    slot_ids = jnp.arange(SLOTS, dtype=jnp.int32)
    picks = inside[:, :, None] & (rank[:, :, None] == slot_ids[None, None, :])
    return jnp.sum(jnp.where(picks, union_blocks[:, :, None] + 1, 0), axis=1) - 1


def combine_stats(top, total, picked):
    n = lax.axis_size("vocab")
    if n & (n - 1):
        stats = lax.all_gather(jnp.stack([top, total, picked]), "vocab")
        best = jnp.max(stats[:, 0], axis=0)
        total = jnp.sum(stats[:, 1] * jnp.exp(stats[:, 0] - best[None, :]), axis=0)
        return best, total, jnp.sum(stats[:, 2], axis=0)
    bit = 1
    while bit < n:
        other = lax.ppermute(
            jnp.stack([top, total, picked]), "vocab", [(k, k ^ bit) for k in range(n)]
        )
        best = jnp.maximum(top, other[0])
        total = total * jnp.exp(top - best) + other[1] * jnp.exp(other[0] - best)
        picked = picked + other[2]
        top = best
        bit *= 2
    return top, total, picked


def halving_scatter(terms, flip=0):
    n = lax.axis_size("vocab")
    if n & (n - 1):
        return lax.psum_scatter(terms, "vocab", scatter_dimension=1, tiled=True)
    me = lax.axis_index("vocab") ^ flip
    rows, width = terms.shape
    part = terms.reshape(rows, n, width // n)
    bit = 1
    while bit < n:
        halves = part.reshape(rows, part.shape[1] // 2, 2, width // n)
        mine = (me // bit) % 2
        keep = lax.dynamic_index_in_dim(halves, mine, 2, keepdims=False)
        send = lax.dynamic_index_in_dim(halves, 1 - mine, 2, keepdims=False)
        got = lax.ppermute(
            send.astype(jnp.bfloat16), "vocab", [(k, k ^ bit) for k in range(n)]
        )
        part = keep + got.astype(jnp.float32)
        bit *= 2
    return part.reshape(rows, width // n)


def doubling_rows(block):
    n = lax.axis_size("vocab")
    if n & (n - 1):
        return lax.all_gather(block, "vocab", axis=1, tiled=True)
    me = lax.axis_index("vocab")
    rows, width = block.shape
    held = block[:, None, :]
    bit = n // 2
    while bit >= 1:
        got = lax.ppermute(held, "vocab", [(k, k ^ bit) for k in range(n)])
        clear = (me // bit) % 2 == 0
        low = jnp.where(clear, held, got)
        high = jnp.where(clear, got, held)
        held = jnp.stack([low, high], axis=2).reshape(rows, 2 * held.shape[1], width)
        bit //= 2
    return held.reshape(rows, n * width)


def doubling_gather(piece):
    n = lax.axis_size("dp")
    if n & (n - 1):
        return lax.all_gather(piece, "dp")
    me = lax.axis_index("dp")
    held = piece[None]
    bit = 1
    while bit < n:
        got = lax.ppermute(held, "dp", [(k, k ^ bit) for k in range(n)])
        low = (me // bit) % 2 == 0
        held = jnp.where(low, jnp.concatenate([held, got]), jnp.concatenate([got, held]))
        bit *= 2
    return held


def shift_exchange(wide, axis):
    n = lax.axis_size("dp")
    me = lax.axis_index("dp")
    own = lax.dynamic_index_in_dim(wide, me, axis, keepdims=True)
    pieces = [own]
    for shift in range(1, n):
        send = lax.dynamic_index_in_dim(wide, (me + shift) % n, axis, keepdims=True)
        pieces.append(lax.ppermute(send, "dp", [(k, (k + shift) % n) for k in range(n)]))
    held = jnp.concatenate(pieces, axis=axis)
    return jnp.take(held, (me - jnp.arange(n)) % n, axis=axis, mode="clip")


def shards(hidden, weight, teacher_ids, teacher_logp, union_blocks):
    tokens_here = hidden.shape[0]
    n_groups = lax.axis_size("dp")
    per_dev = weight.shape[0] // BLOCK
    piece = weight.shape[1]
    width = SLOTS * BLOCK
    dp_row = lax.axis_index("dp")
    column = lax.axis_index("vocab")
    table = slot_table(union_blocks, column, per_dev)
    filled = table >= 0
    local = jnp.where(filled, table - column * per_dev, -1)
    blocks = weight.reshape(per_dev, BLOCK, piece)
    chosen = jnp.take(blocks, jnp.maximum(local, 0).reshape(-1), axis=0, mode="clip").reshape(
        n_groups, width, piece
    )
    full_rows = doubling_rows(hidden)
    wide = full_rows.reshape(tokens_here, n_groups, piece)
    n_vocab = lax.axis_size("vocab")
    pair = n_groups == 2 and n_vocab % 2 == 0 and not n_vocab & (n_vocab - 1)
    if pair:
        own_half = lax.dynamic_index_in_dim(wide, dp_row, 1, keepdims=False)
        other_half = lax.dynamic_index_in_dim(wide, 1 - dp_row, 1, keepdims=False)
        got_half = lax.ppermute(other_half, "dp", [(0, 1), (1, 0)])
    else:
        halves = shift_exchange(wide, 1)
    own_slots = lax.dynamic_index_in_dim(table, dp_row, 0, keepdims=False)
    col_mask = jnp.repeat(own_slots >= 0, BLOCK)
    if pair:
        slot_rows = jnp.maximum(local, 0)

        def rows_of(tile):
            picks = lax.dynamic_index_in_dim(slot_rows, tile, 0, keepdims=False)
            return jnp.take(blocks, picks, axis=0, mode="clip").reshape(width, piece)

        got_w = lax.ppermute(rows_of(1 - dp_row), "dp", [(0, 1), (1, 0)])
        own_w = rows_of(dp_row)
        held_w = jnp.stack([own_w, got_w])
    else:
        rows_w = shift_exchange(chosen, 0)
    if pair:
        logits = jnp.einsum(
            "td,rd->tr", own_half, own_w, preferred_element_type=jnp.float32
        ) + jnp.einsum("td,rd->tr", other_half, got_w, preferred_element_type=jnp.float32)
    else:
        logits = jnp.einsum("tkd,krd->tr", wide, rows_w, preferred_element_type=jnp.float32)
    offsets = teacher_ids % BLOCK
    match = (teacher_ids // BLOCK)[:, :, None] == own_slots[None, None, :]
    starts = jnp.arange(SLOTS, dtype=jnp.int32) * BLOCK
    position = jnp.sum(jnp.where(match, starts[None, None, :] + offsets[:, :, None], 0), axis=-1)
    hit = jnp.any(match, axis=-1)
    teacher_q = jax.nn.softmax(teacher_logp, axis=-1) * hit.astype(jnp.float32)
    onehot = (position[:, :, None] == jnp.arange(width, dtype=jnp.int32)[None, None, :]).astype(
        jnp.float32
    )
    target = jnp.einsum("tk,tkr->tr", teacher_q, onehot)
    masked = jnp.where(col_mask[None, :], logits, negative)
    local_top = jnp.max(masked, axis=1)
    aimed = jnp.sum(target * logits, axis=1)
    local_total = jnp.sum(jnp.where(col_mask[None, :], jnp.exp(masked - local_top[:, None]), 0.0), axis=1)
    top, total, picked = combine_stats(local_top, local_total, aimed)
    lse = top + jnp.log(total)
    loss = lse - picked
    probs = jnp.where(col_mask[None, :], jnp.exp(logits - lse[:, None]), 0.0)
    dlog = (probs - target).astype(jnp.bfloat16)
    if pair:
        hidden_terms = jnp.einsum("tr,krd->tkd", dlog, held_w, preferred_element_type=jnp.float32)
        flip = dp_row * (lax.axis_size("vocab") // 2)
    else:
        hidden_terms = jnp.einsum("tr,krd->tkd", dlog, rows_w, preferred_element_type=jnp.float32)
        flip = 0
    hidden_terms = hidden_terms.reshape(tokens_here, n_groups * piece)
    grad_hidden = halving_scatter(hidden_terms, flip).astype(jnp.bfloat16)
    dlog_all = doubling_gather(dlog).reshape(n_groups, tokens_here, SLOTS, BLOCK)
    block_ids = jnp.arange(per_dev, dtype=jnp.int32)
    placed = jnp.zeros((n_groups, tokens_here, per_dev, BLOCK), jnp.bfloat16)
    for q in range(SLOTS):
        hit_q = local[:, q][:, None] == block_ids[None, :]
        placed = placed + jnp.where(
            hit_q[:, None, :, None], dlog_all[:, :, q, :][:, :, None, :], jnp.zeros((), jnp.bfloat16)
        )
    placed = placed.reshape(n_groups, tokens_here, per_dev * BLOCK)
    grad_weight = weight_grad(pair, placed, dp_row, halves if not pair else None,
                              (own_half, got_half) if pair else None)
    return (loss, grad_hidden, grad_weight)


def weight_grad(pair, placed, dp_row, halves, pieces):
    if pair:
        own_half, got_half = pieces
        mine_p = lax.dynamic_index_in_dim(placed, dp_row, 0, keepdims=False)
        other_p = lax.dynamic_index_in_dim(placed, 1 - dp_row, 0, keepdims=False)
        grad_weight = jnp.einsum(
            "tr,td->rd",
            jnp.concatenate([mine_p, other_p]),
            jnp.concatenate([own_half, got_half]),
            preferred_element_type=jnp.float32,
        ).astype(jnp.bfloat16)
    else:
        grad_weight = jnp.einsum(
            "str,tsd->rd", placed, halves, preferred_element_type=jnp.float32
        ).astype(jnp.bfloat16)
    return grad_weight


def solution(mesh):
    return jax.shard_map(
        shards,
        mesh=mesh,
        in_specs=(P("dp", "vocab"), P("vocab", "dp"), P("dp", None), P("dp", None), P()),
        out_specs=(P("dp"), P("dp", "vocab"), P("vocab", "dp")),
        check_vma=False,
    )
```

```python
import jax
import jax.numpy as jnp
from jax import lax
from jax.sharding import PartitionSpec as P

BLOCK = 128
SLOTS = 2


negative = -1e30


def slot_table(union_blocks, column, per_dev):
    inside = union_blocks // per_dev == column
    rank = jnp.cumsum(inside.astype(jnp.int32), axis=1) - 1
    slot_ids = jnp.arange(SLOTS, dtype=jnp.int32)
    picks = inside[:, :, None] & (rank[:, :, None] == slot_ids[None, None, :])
    return jnp.sum(jnp.where(picks, union_blocks[:, :, None] + 1, 0), axis=1) - 1


def combine_stats(top, total, picked):
    n = lax.axis_size("vocab")
    if n & (n - 1):
        stats = lax.all_gather(jnp.stack([top, total, picked]), "vocab")
        best = jnp.max(stats[:, 0], axis=0)
        total = jnp.sum(stats[:, 1] * jnp.exp(stats[:, 0] - best[None, :]), axis=0)
        return best, total, jnp.sum(stats[:, 2], axis=0)
    bit = 1
    while bit < n:
        other = lax.ppermute(
            jnp.stack([top, total, picked]), "vocab", [(k, k ^ bit) for k in range(n)]
        )
        best = jnp.maximum(top, other[0])
        total = total * jnp.exp(top - best) + other[1] * jnp.exp(other[0] - best)
        picked = picked + other[2]
        top = best
        bit *= 2
    return top, total, picked


def halving_scatter(terms, flip=0):
    n = lax.axis_size("vocab")
    if n & (n - 1):
        return lax.psum_scatter(terms, "vocab", scatter_dimension=1, tiled=True)
    me = lax.axis_index("vocab") ^ flip
    rows, width = terms.shape
    part = terms.reshape(rows, n, width // n)
    bit = 1
    while bit < n:
        halves = part.reshape(rows, part.shape[1] // 2, 2, width // n)
        low = (me // bit) % 2 == 0
        keep = jnp.where(low, halves[:, :, 0], halves[:, :, 1])
        send = jnp.where(low, halves[:, :, 1], halves[:, :, 0])
        got = lax.ppermute(
            send.astype(jnp.bfloat16), "vocab", [(k, k ^ bit) for k in range(n)]
        )
        part = keep + got.astype(jnp.float32)
        bit *= 2
    return part.reshape(rows, width // n)


def doubling_rows(block):
    n = lax.axis_size("vocab")
    if n & (n - 1):
        return lax.all_gather(block, "vocab", axis=1, tiled=True)
    me = lax.axis_index("vocab")
    rows, width = block.shape
    held = block[:, None, :]
    bit = n // 2
    while bit >= 1:
        got = lax.ppermute(held, "vocab", [(k, k ^ bit) for k in range(n)])
        clear = (me // bit) % 2 == 0
        low = jnp.where(clear, held, got)
        high = jnp.where(clear, got, held)
        held = jnp.stack([low, high], axis=2).reshape(rows, 2 * held.shape[1], width)
        bit //= 2
    return held.reshape(rows, n * width)


def doubling_gather(piece):
    n = lax.axis_size("dp")
    if n & (n - 1):
        return lax.all_gather(piece, "dp")
    me = lax.axis_index("dp")
    held = piece[None]
    bit = 1
    while bit < n:
        got = lax.ppermute(held, "dp", [(k, k ^ bit) for k in range(n)])
        low = (me // bit) % 2 == 0
        held = jnp.where(low, jnp.concatenate([held, got]), jnp.concatenate([got, held]))
        bit *= 2
    return held


def shift_exchange(wide, axis):
    n = lax.axis_size("dp")
    me = lax.axis_index("dp")
    own = lax.dynamic_index_in_dim(wide, me, axis, keepdims=True)
    pieces = [own]
    for shift in range(1, n):
        send = lax.dynamic_index_in_dim(wide, (me + shift) % n, axis, keepdims=True)
        pieces.append(lax.ppermute(send, "dp", [(k, (k + shift) % n) for k in range(n)]))
    held = jnp.concatenate(pieces, axis=axis)
    return jnp.take(held, (me - jnp.arange(n)) % n, axis=axis, mode="clip")


def shards(hidden, weight, teacher_ids, teacher_logp, union_blocks):
    tokens_here = hidden.shape[0]
    n_groups = lax.axis_size("dp")
    per_dev = weight.shape[0] // BLOCK
    piece = weight.shape[1]
    width = SLOTS * BLOCK
    dp_row = lax.axis_index("dp")
    column = lax.axis_index("vocab")
    table = slot_table(union_blocks, column, per_dev)
    filled = table >= 0
    local = jnp.where(filled, table - column * per_dev, -1)
    blocks = weight.reshape(per_dev, BLOCK, piece)
    chosen = jnp.take(blocks, jnp.maximum(local, 0).reshape(-1), axis=0, mode="clip").reshape(
        n_groups, width, piece
    )
    full_rows = doubling_rows(hidden)
    wide = full_rows.reshape(tokens_here, n_groups, piece)
    n_vocab = lax.axis_size("vocab")
    pair = n_groups == 2 and n_vocab % 2 == 0 and not n_vocab & (n_vocab - 1)
    if pair:
        own_half = lax.dynamic_index_in_dim(wide, dp_row, 1, keepdims=False)
        other_half = lax.dynamic_index_in_dim(wide, 1 - dp_row, 1, keepdims=False)
        got_half = lax.ppermute(other_half, "dp", [(0, 1), (1, 0)])
    else:
        halves = shift_exchange(wide, 1)
    own_slots = lax.dynamic_index_in_dim(table, dp_row, 0, keepdims=False)
    col_mask = jnp.repeat(own_slots >= 0, BLOCK)
    if pair:
        slot_rows = jnp.maximum(local, 0)

        def rows_of(tile):
            picks = lax.dynamic_index_in_dim(slot_rows, tile, 0, keepdims=False)
            return jnp.take(blocks, picks, axis=0, mode="clip").reshape(width, piece)

        got_w = lax.ppermute(rows_of(1 - dp_row), "dp", [(0, 1), (1, 0)])
        own_w = rows_of(dp_row)
        held_w = jnp.stack([own_w, got_w])
    else:
        rows_w = shift_exchange(chosen, 0)
    if pair:
        logits = jnp.einsum(
            "td,rd->tr", own_half, own_w, preferred_element_type=jnp.float32
        ) + jnp.einsum("td,rd->tr", other_half, got_w, preferred_element_type=jnp.float32)
    else:
        logits = jnp.einsum("tkd,krd->tr", wide, rows_w, preferred_element_type=jnp.float32)
    offsets = teacher_ids % BLOCK
    match = (teacher_ids // BLOCK)[:, :, None] == own_slots[None, None, :]
    starts = jnp.arange(SLOTS, dtype=jnp.int32) * BLOCK
    position = jnp.sum(jnp.where(match, starts[None, None, :] + offsets[:, :, None], 0), axis=-1)
    hit = jnp.any(match, axis=-1)
    teacher_q = jax.nn.softmax(teacher_logp, axis=-1) * hit.astype(jnp.float32)
    onehot = (position[:, :, None] == jnp.arange(width, dtype=jnp.int32)[None, None, :]).astype(
        jnp.float32
    )
    target = jnp.einsum("tk,tkr->tr", teacher_q, onehot)
    masked = jnp.where(col_mask[None, :], logits, negative)
    local_top = jnp.max(masked, axis=1)
    aimed = jnp.sum(target * logits, axis=1)
    local_total = jnp.sum(jnp.where(col_mask[None, :], jnp.exp(masked - local_top[:, None]), 0.0), axis=1)
    top, total, picked = combine_stats(local_top, local_total, aimed)
    lse = top + jnp.log(total)
    loss = lse - picked
    probs = jnp.where(col_mask[None, :], jnp.exp(logits - lse[:, None]), 0.0)
    dlog = (probs - target).astype(jnp.bfloat16)
    if pair:
        hidden_terms = jnp.einsum("tr,krd->tkd", dlog, held_w, preferred_element_type=jnp.float32)
        flip = dp_row * (lax.axis_size("vocab") // 2)
    else:
        hidden_terms = jnp.einsum("tr,krd->tkd", dlog, rows_w, preferred_element_type=jnp.float32)
        flip = 0
    hidden_terms = hidden_terms.reshape(tokens_here, n_groups * piece)
    grad_hidden = halving_scatter(hidden_terms, flip).astype(jnp.bfloat16)
    dlog_all = doubling_gather(dlog).reshape(n_groups, tokens_here, SLOTS, BLOCK)
    block_ids = jnp.arange(per_dev, dtype=jnp.int32)
    placed = jnp.zeros((n_groups, tokens_here, per_dev, BLOCK), jnp.bfloat16)
    for q in range(SLOTS):
        hit_q = local[:, q][:, None] == block_ids[None, :]
        placed = placed + jnp.where(
            hit_q[:, None, :, None], dlog_all[:, :, q, :][:, :, None, :], jnp.zeros((), jnp.bfloat16)
        )
    placed = placed.reshape(n_groups, tokens_here, per_dev * BLOCK)
    grad_weight = weight_grad(pair, placed, dp_row, halves if not pair else None,
                              (own_half, got_half) if pair else None)
    return (loss, grad_hidden, grad_weight)


def weight_grad(pair, placed, dp_row, halves, pieces):
    if pair:
        own_half, got_half = pieces
        mine_p = lax.dynamic_index_in_dim(placed, dp_row, 0, keepdims=False)
        other_p = lax.dynamic_index_in_dim(placed, 1 - dp_row, 0, keepdims=False)
        grad_weight = jnp.einsum(
            "tr,td->rd",
            jnp.concatenate([mine_p, other_p]),
            jnp.concatenate([own_half, got_half]),
            preferred_element_type=jnp.float32,
        ).astype(jnp.bfloat16)
    else:
        grad_weight = jnp.einsum(
            "str,tsd->rd", placed, halves, preferred_element_type=jnp.float32
        ).astype(jnp.bfloat16)
    return grad_weight


def solution(mesh):
    return jax.shard_map(
        shards,
        mesh=mesh,
        in_specs=(P("dp", "vocab"), P("vocab", "dp"), P("dp", None), P("dp", None), P()),
        out_specs=(P("dp"), P("dp", "vocab"), P("vocab", "dp")),
        check_vma=False,
    )
```

```python
import jax
import jax.numpy as jnp
from jax import lax
from jax.sharding import PartitionSpec as P

BLOCK = 128
SLOTS = 2


negative = -1e30


def slot_table(union_blocks, column, per_dev):
    inside = union_blocks // per_dev == column
    rank = jnp.cumsum(inside.astype(jnp.int32), axis=1) - 1
    slot_ids = jnp.arange(SLOTS, dtype=jnp.int32)
    picks = inside[:, :, None] & (rank[:, :, None] == slot_ids[None, None, :])
    return jnp.sum(jnp.where(picks, union_blocks[:, :, None] + 1, 0), axis=1) - 1


def combine_stats(top, total, picked):
    n = lax.axis_size("vocab")
    if n & (n - 1):
        stats = lax.all_gather(jnp.stack([top, total, picked]), "vocab")
        best = jnp.max(stats[:, 0], axis=0)
        total = jnp.sum(stats[:, 1] * jnp.exp(stats[:, 0] - best[None, :]), axis=0)
        return best, total, jnp.sum(stats[:, 2], axis=0)
    bit = 1
    while bit < n:
        other = lax.ppermute(
            jnp.stack([top, total, picked]), "vocab", [(k, k ^ bit) for k in range(n)]
        )
        best = jnp.maximum(top, other[0])
        total = total * jnp.exp(top - best) + other[1] * jnp.exp(other[0] - best)
        picked = picked + other[2]
        top = best
        bit *= 2
    return top, total, picked


def halving_scatter(terms, flip=0):
    n = lax.axis_size("vocab")
    if n & (n - 1):
        return lax.psum_scatter(terms, "vocab", scatter_dimension=1, tiled=True)
    me = lax.axis_index("vocab") ^ flip
    rows, width = terms.shape
    part = terms.reshape(rows, n, width // n)
    bit = 1
    while bit < n:
        halves = part.reshape(rows, part.shape[1] // 2, 2, width // n)
        low = (me // bit) % 2 == 0
        keep = jnp.where(low, halves[:, :, 0], halves[:, :, 1])
        send = jnp.where(low, halves[:, :, 1], halves[:, :, 0])
        got = lax.ppermute(
            send.astype(jnp.bfloat16), "vocab", [(k, k ^ bit) for k in range(n)]
        )
        part = keep + got.astype(jnp.float32)
        bit *= 2
    return part.reshape(rows, width // n)


def doubling_rows(block):
    n = lax.axis_size("vocab")
    if n & (n - 1):
        return lax.all_gather(block, "vocab", axis=1, tiled=True)
    me = lax.axis_index("vocab")
    rows, width = block.shape
    held = block[:, None, :]
    bit = n // 2
    while bit >= 1:
        got = lax.ppermute(held, "vocab", [(k, k ^ bit) for k in range(n)])
        clear = (me // bit) % 2 == 0
        low = jnp.where(clear, held, got)
        high = jnp.where(clear, got, held)
        held = jnp.stack([low, high], axis=2).reshape(rows, 2 * held.shape[1], width)
        bit //= 2
    return held.reshape(rows, n * width)


def doubling_gather(piece):
    n = lax.axis_size("dp")
    if n & (n - 1):
        return lax.all_gather(piece, "dp")
    me = lax.axis_index("dp")
    held = piece[None]
    bit = 1
    while bit < n:
        got = lax.ppermute(held, "dp", [(k, k ^ bit) for k in range(n)])
        low = (me // bit) % 2 == 0
        held = jnp.where(low, jnp.concatenate([held, got]), jnp.concatenate([got, held]))
        bit *= 2
    return held


def shift_exchange(wide, axis):
    n = lax.axis_size("dp")
    me = lax.axis_index("dp")
    own = lax.dynamic_index_in_dim(wide, me, axis, keepdims=True)
    pieces = [own]
    for shift in range(1, n):
        send = lax.dynamic_index_in_dim(wide, (me + shift) % n, axis, keepdims=True)
        pieces.append(lax.ppermute(send, "dp", [(k, (k + shift) % n) for k in range(n)]))
    held = jnp.concatenate(pieces, axis=axis)
    return jnp.take(held, (me - jnp.arange(n)) % n, axis=axis, mode="clip")


def shards(hidden, weight, teacher_ids, teacher_logp, union_blocks):
    tokens_here = hidden.shape[0]
    n_groups = lax.axis_size("dp")
    per_dev = weight.shape[0] // BLOCK
    piece = weight.shape[1]
    width = SLOTS * BLOCK
    dp_row = lax.axis_index("dp")
    column = lax.axis_index("vocab")
    table = slot_table(union_blocks, column, per_dev)
    filled = table >= 0
    local = jnp.where(filled, table - column * per_dev, -1)
    blocks = weight.reshape(per_dev, BLOCK, piece)
    chosen = jnp.take(blocks, jnp.maximum(local, 0).reshape(-1), axis=0, mode="clip").reshape(
        n_groups, width, piece
    )
    full_rows = doubling_rows(hidden)
    wide = full_rows.reshape(tokens_here, n_groups, piece)
    n_vocab = lax.axis_size("vocab")
    pair = n_groups == 2 and n_vocab % 2 == 0 and not n_vocab & (n_vocab - 1)
    if pair:
        first = dp_row == 0
        own_half = jnp.where(first, wide[:, 0], wide[:, 1])
        other_half = jnp.where(first, wide[:, 1], wide[:, 0])
        got_half = lax.ppermute(other_half, "dp", [(0, 1), (1, 0)])
    else:
        halves = shift_exchange(wide, 1)
    own_slots = lax.dynamic_index_in_dim(table, dp_row, 0, keepdims=False)
    col_mask = jnp.repeat(own_slots >= 0, BLOCK)
    if pair:
        slot_rows = jnp.maximum(local, 0)

        def rows_of(tile):
            picks = lax.dynamic_index_in_dim(slot_rows, tile, 0, keepdims=False)
            return jnp.take(blocks, picks, axis=0, mode="clip").reshape(width, piece)

        got_w = lax.ppermute(rows_of(1 - dp_row), "dp", [(0, 1), (1, 0)])
        own_w = rows_of(dp_row)
        held_w = jnp.stack([own_w, got_w])
    else:
        rows_w = shift_exchange(chosen, 0)
    if pair:
        logits = jnp.einsum(
            "td,rd->tr", own_half, own_w, preferred_element_type=jnp.float32
        ) + jnp.einsum("td,rd->tr", other_half, got_w, preferred_element_type=jnp.float32)
    else:
        logits = jnp.einsum("tkd,krd->tr", wide, rows_w, preferred_element_type=jnp.float32)
    offsets = teacher_ids % BLOCK
    match = (teacher_ids // BLOCK)[:, :, None] == own_slots[None, None, :]
    starts = jnp.arange(SLOTS, dtype=jnp.int32) * BLOCK
    position = jnp.sum(jnp.where(match, starts[None, None, :] + offsets[:, :, None], 0), axis=-1)
    hit = jnp.any(match, axis=-1)
    teacher_q = jax.nn.softmax(teacher_logp, axis=-1) * hit.astype(jnp.float32)
    onehot = (position[:, :, None] == jnp.arange(width, dtype=jnp.int32)[None, None, :]).astype(
        jnp.float32
    )
    target = jnp.einsum("tk,tkr->tr", teacher_q, onehot)
    masked = jnp.where(col_mask[None, :], logits, negative)
    local_top = jnp.max(masked, axis=1)
    aimed = jnp.sum(target * logits, axis=1)
    local_total = jnp.sum(jnp.where(col_mask[None, :], jnp.exp(masked - local_top[:, None]), 0.0), axis=1)
    top, total, picked = combine_stats(local_top, local_total, aimed)
    lse = top + jnp.log(total)
    loss = lse - picked
    probs = jnp.where(col_mask[None, :], jnp.exp(logits - lse[:, None]), 0.0)
    dlog = (probs - target).astype(jnp.bfloat16)
    if pair:
        hidden_terms = jnp.einsum("tr,krd->tkd", dlog, held_w, preferred_element_type=jnp.float32)
        flip = dp_row * (lax.axis_size("vocab") // 2)
    else:
        hidden_terms = jnp.einsum("tr,krd->tkd", dlog, rows_w, preferred_element_type=jnp.float32)
        flip = 0
    hidden_terms = hidden_terms.reshape(tokens_here, n_groups * piece)
    grad_hidden = halving_scatter(hidden_terms, flip).astype(jnp.bfloat16)
    dlog_all = doubling_gather(dlog).reshape(n_groups, tokens_here, SLOTS, BLOCK)
    block_ids = jnp.arange(per_dev, dtype=jnp.int32)
    placed = jnp.zeros((n_groups, tokens_here, per_dev, BLOCK), jnp.bfloat16)
    for q in range(SLOTS):
        hit_q = local[:, q][:, None] == block_ids[None, :]
        placed = placed + jnp.where(
            hit_q[:, None, :, None], dlog_all[:, :, q, :][:, :, None, :], jnp.zeros((), jnp.bfloat16)
        )
    placed = placed.reshape(n_groups, tokens_here, per_dev * BLOCK)
    grad_weight = weight_grad(pair, placed, dp_row, halves if not pair else None,
                              (own_half, got_half) if pair else None)
    return (loss, grad_hidden, grad_weight)


def weight_grad(pair, placed, dp_row, halves, pieces):
    if pair:
        own_half, got_half = pieces
        mine_p = jnp.where(dp_row == 0, placed[0], placed[1])
        other_p = jnp.where(dp_row == 0, placed[1], placed[0])
        grad_weight = jnp.einsum(
            "tr,td->rd",
            jnp.concatenate([mine_p, other_p]),
            jnp.concatenate([own_half, got_half]),
            preferred_element_type=jnp.float32,
        ).astype(jnp.bfloat16)
    else:
        grad_weight = jnp.einsum(
            "str,tsd->rd", placed, halves, preferred_element_type=jnp.float32
        ).astype(jnp.bfloat16)
    return grad_weight


def solution(mesh):
    return jax.shard_map(
        shards,
        mesh=mesh,
        in_specs=(P("dp", "vocab"), P("vocab", "dp"), P("dp", None), P("dp", None), P()),
        out_specs=(P("dp"), P("dp", "vocab"), P("vocab", "dp")),
        check_vma=False,
    )
```

```python
import jax
import jax.numpy as jnp
from jax import lax
from jax.sharding import PartitionSpec as P

BLOCK = 128
SLOTS = 2


negative = -1e30


def slot_table(union_blocks, column, per_dev):
    inside = union_blocks // per_dev == column
    rank = jnp.cumsum(inside.astype(jnp.int32), axis=1) - 1
    slot_ids = jnp.arange(SLOTS, dtype=jnp.int32)
    picks = inside[:, :, None] & (rank[:, :, None] == slot_ids[None, None, :])
    return jnp.sum(jnp.where(picks, union_blocks[:, :, None] + 1, 0), axis=1) - 1


def combine_stats(top, total, picked):
    n = lax.axis_size("vocab")
    if n & (n - 1):
        stats = lax.all_gather(jnp.stack([top, total, picked]), "vocab")
        best = jnp.max(stats[:, 0], axis=0)
        total = jnp.sum(stats[:, 1] * jnp.exp(stats[:, 0] - best[None, :]), axis=0)
        return best, total, jnp.sum(stats[:, 2], axis=0)
    bit = 1
    while bit < n:
        other = lax.ppermute(
            jnp.stack([top, total, picked]), "vocab", [(k, k ^ bit) for k in range(n)]
        )
        best = jnp.maximum(top, other[0])
        total = total * jnp.exp(top - best) + other[1] * jnp.exp(other[0] - best)
        picked = picked + other[2]
        top = best
        bit *= 2
    return top, total, picked


def halving_scatter(terms, flip=0):
    n = lax.axis_size("vocab")
    if n & (n - 1):
        return lax.psum_scatter(terms, "vocab", scatter_dimension=1, tiled=True)
    me = lax.axis_index("vocab") ^ flip
    rows, width = terms.shape
    part = terms.reshape(rows, n, width // n)
    bit = 1
    while bit < n:
        halves = part.reshape(rows, part.shape[1] // 2, 2, width // n)
        low = (me // bit) % 2 == 0
        keep = jnp.where(low, halves[:, :, 0], halves[:, :, 1])
        send = jnp.where(low, halves[:, :, 1], halves[:, :, 0])
        got = lax.ppermute(
            send.astype(jnp.bfloat16), "vocab", [(k, k ^ bit) for k in range(n)]
        )
        part = keep + got.astype(jnp.float32)
        bit *= 2
    return part.reshape(rows, width // n)


def doubling_rows(block):
    n = lax.axis_size("vocab")
    if n & (n - 1):
        return lax.all_gather(block, "vocab", axis=1, tiled=True)
    me = lax.axis_index("vocab")
    rows, width = block.shape
    held = block[:, None, :]
    bit = n // 2
    while bit >= 1:
        got = lax.ppermute(held, "vocab", [(k, k ^ bit) for k in range(n)])
        clear = (me // bit) % 2 == 0
        low = jnp.where(clear, held, got)
        high = jnp.where(clear, got, held)
        held = jnp.stack([low, high], axis=2).reshape(rows, 2 * held.shape[1], width)
        bit //= 2
    return held.reshape(rows, n * width)


def doubling_gather(piece):
    n = lax.axis_size("dp")
    if n & (n - 1):
        return lax.all_gather(piece, "dp")
    me = lax.axis_index("dp")
    held = piece[None]
    bit = 1
    while bit < n:
        got = lax.ppermute(held, "dp", [(k, k ^ bit) for k in range(n)])
        low = (me // bit) % 2 == 0
        held = jnp.where(low, jnp.concatenate([held, got]), jnp.concatenate([got, held]))
        bit *= 2
    return held


def shift_exchange(wide, axis):
    n = lax.axis_size("dp")
    me = lax.axis_index("dp")
    own = lax.dynamic_index_in_dim(wide, me, axis, keepdims=True)
    pieces = [own]
    for shift in range(1, n):
        send = lax.dynamic_index_in_dim(wide, (me + shift) % n, axis, keepdims=True)
        pieces.append(lax.ppermute(send, "dp", [(k, (k + shift) % n) for k in range(n)]))
    held = jnp.concatenate(pieces, axis=axis)
    return jnp.take(held, (me - jnp.arange(n)) % n, axis=axis, mode="clip")


def shards(hidden, weight, teacher_ids, teacher_logp, union_blocks):
    tokens_here = hidden.shape[0]
    n_groups = lax.axis_size("dp")
    per_dev = weight.shape[0] // BLOCK
    piece = weight.shape[1]
    width = SLOTS * BLOCK
    dp_row = lax.axis_index("dp")
    column = lax.axis_index("vocab")
    table = slot_table(union_blocks, column, per_dev)
    filled = table >= 0
    local = jnp.where(filled, table - column * per_dev, -1)
    blocks = weight.reshape(per_dev, BLOCK, piece)
    chosen = jnp.take(blocks, jnp.maximum(local, 0).reshape(-1), axis=0, mode="clip").reshape(
        n_groups, width, piece
    )
    full_rows = doubling_rows(hidden)
    wide = full_rows.reshape(tokens_here, n_groups, piece)
    n_vocab = lax.axis_size("vocab")
    pair = n_groups == 2 and n_vocab % 2 == 0 and not n_vocab & (n_vocab - 1)
    if pair:
        first = dp_row == 0
        own_half = jnp.where(first, wide[:, 0], wide[:, 1])
        other_half = jnp.where(first, wide[:, 1], wide[:, 0])
        got_half = lax.ppermute(other_half, "dp", [(0, 1), (1, 0)])
    else:
        halves = shift_exchange(wide, 1)
    own_slots = lax.dynamic_index_in_dim(table, dp_row, 0, keepdims=False)
    col_mask = jnp.repeat(own_slots >= 0, BLOCK)
    if pair:
        slot_rows = jnp.maximum(local, 0)

        def rows_of(tile):
            picks = lax.dynamic_index_in_dim(slot_rows, tile, 0, keepdims=False)
            return jnp.take(blocks, picks, axis=0, mode="clip").reshape(width, piece)

        partner_slots = lax.dynamic_index_in_dim(slot_rows, 1 - dp_row, 0, keepdims=False)
        got_w = jnp.concatenate([
            lax.ppermute(
                lax.dynamic_index_in_dim(blocks, partner_slots[q], 0, keepdims=False),
                "dp",
                [(0, 1), (1, 0)],
            )
            for q in range(SLOTS)
        ])
        own_w = rows_of(dp_row)
        held_w = jnp.stack([own_w, got_w])
    else:
        rows_w = shift_exchange(chosen, 0)
    if pair:
        logits = jnp.einsum(
            "td,rd->tr", own_half, own_w, preferred_element_type=jnp.float32
        ) + jnp.einsum("td,rd->tr", other_half, got_w, preferred_element_type=jnp.float32)
    else:
        logits = jnp.einsum("tkd,krd->tr", wide, rows_w, preferred_element_type=jnp.float32)
    offsets = teacher_ids % BLOCK
    match = (teacher_ids // BLOCK)[:, :, None] == own_slots[None, None, :]
    starts = jnp.arange(SLOTS, dtype=jnp.int32) * BLOCK
    position = jnp.sum(jnp.where(match, starts[None, None, :] + offsets[:, :, None], 0), axis=-1)
    hit = jnp.any(match, axis=-1)
    teacher_q = jax.nn.softmax(teacher_logp, axis=-1) * hit.astype(jnp.float32)
    onehot = (position[:, :, None] == jnp.arange(width, dtype=jnp.int32)[None, None, :]).astype(
        jnp.float32
    )
    target = jnp.einsum("tk,tkr->tr", teacher_q, onehot)
    masked = jnp.where(col_mask[None, :], logits, negative)
    local_top = jnp.max(masked, axis=1)
    aimed = jnp.sum(target * logits, axis=1)
    local_total = jnp.sum(jnp.where(col_mask[None, :], jnp.exp(masked - local_top[:, None]), 0.0), axis=1)
    top, total, picked = combine_stats(local_top, local_total, aimed)
    lse = top + jnp.log(total)
    loss = lse - picked
    probs = jnp.where(col_mask[None, :], jnp.exp(logits - lse[:, None]), 0.0)
    dlog = (probs - target).astype(jnp.bfloat16)
    if pair:
        hidden_terms = jnp.einsum("tr,krd->tkd", dlog, held_w, preferred_element_type=jnp.float32)
        flip = dp_row * (lax.axis_size("vocab") // 2)
    else:
        hidden_terms = jnp.einsum("tr,krd->tkd", dlog, rows_w, preferred_element_type=jnp.float32)
        flip = 0
    hidden_terms = hidden_terms.reshape(tokens_here, n_groups * piece)
    grad_hidden = halving_scatter(hidden_terms, flip).astype(jnp.bfloat16)
    dlog_all = doubling_gather(dlog).reshape(n_groups, tokens_here, SLOTS, BLOCK)
    block_ids = jnp.arange(per_dev, dtype=jnp.int32)
    placed = jnp.zeros((n_groups, tokens_here, per_dev, BLOCK), jnp.bfloat16)
    for q in range(SLOTS):
        hit_q = local[:, q][:, None] == block_ids[None, :]
        placed = placed + jnp.where(
            hit_q[:, None, :, None], dlog_all[:, :, q, :][:, :, None, :], jnp.zeros((), jnp.bfloat16)
        )
    placed = placed.reshape(n_groups, tokens_here, per_dev * BLOCK)
    grad_weight = weight_grad(pair, placed, dp_row, halves if not pair else None,
                              (own_half, got_half) if pair else None)
    return (loss, grad_hidden, grad_weight)


def weight_grad(pair, placed, dp_row, halves, pieces):
    if pair:
        own_half, got_half = pieces
        mine_p = jnp.where(dp_row == 0, placed[0], placed[1])
        other_p = jnp.where(dp_row == 0, placed[1], placed[0])
        grad_weight = jnp.einsum(
            "tr,td->rd",
            jnp.concatenate([mine_p, other_p]),
            jnp.concatenate([own_half, got_half]),
            preferred_element_type=jnp.float32,
        ).astype(jnp.bfloat16)
    else:
        grad_weight = jnp.einsum(
            "str,tsd->rd", placed, halves, preferred_element_type=jnp.float32
        ).astype(jnp.bfloat16)
    return grad_weight


def solution(mesh):
    return jax.shard_map(
        shards,
        mesh=mesh,
        in_specs=(P("dp", "vocab"), P("vocab", "dp"), P("dp", None), P("dp", None), P()),
        out_specs=(P("dp"), P("dp", "vocab"), P("vocab", "dp")),
        check_vma=False,
    )
```

```python
import jax
import jax.numpy as jnp
from jax import lax
from jax.sharding import PartitionSpec as P

BLOCK = 128
SLOTS = 2


negative = -1e30


def slot_table(union_blocks, column, per_dev):
    inside = union_blocks // per_dev == column
    rank = jnp.cumsum(inside.astype(jnp.int32), axis=1) - 1
    slot_ids = jnp.arange(SLOTS, dtype=jnp.int32)
    picks = inside[:, :, None] & (rank[:, :, None] == slot_ids[None, None, :])
    return jnp.sum(jnp.where(picks, union_blocks[:, :, None] + 1, 0), axis=1) - 1


def combine_stats(top, total, picked):
    n = lax.axis_size("vocab")
    if n & (n - 1):
        stats = lax.all_gather(jnp.stack([top, total, picked]), "vocab")
        best = jnp.max(stats[:, 0], axis=0)
        total = jnp.sum(stats[:, 1] * jnp.exp(stats[:, 0] - best[None, :]), axis=0)
        return best, total, jnp.sum(stats[:, 2], axis=0)
    bit = 1
    while bit < n:
        other = lax.ppermute(
            jnp.stack([top, total, picked]), "vocab", [(k, k ^ bit) for k in range(n)]
        )
        best = jnp.maximum(top, other[0])
        total = total * jnp.exp(top - best) + other[1] * jnp.exp(other[0] - best)
        picked = picked + other[2]
        top = best
        bit *= 2
    return top, total, picked


def halving_scatter(terms, flip=0):
    n = lax.axis_size("vocab")
    if n & (n - 1):
        return lax.psum_scatter(terms, "vocab", scatter_dimension=1, tiled=True)
    me = lax.axis_index("vocab") ^ flip
    rows, width = terms.shape
    part = terms.reshape(rows, n, width // n)
    bit = 1
    while bit < n:
        halves = part.reshape(rows, part.shape[1] // 2, 2, width // n)
        low = (me // bit) % 2 == 0
        keep = jnp.where(low, halves[:, :, 0], halves[:, :, 1])
        send = jnp.where(low, halves[:, :, 1], halves[:, :, 0])
        got = lax.ppermute(
            send.astype(jnp.bfloat16), "vocab", [(k, k ^ bit) for k in range(n)]
        )
        part = keep + got.astype(jnp.float32)
        bit *= 2
    return part.reshape(rows, width // n)


def doubling_rows(block):
    n = lax.axis_size("vocab")
    if n & (n - 1):
        return lax.all_gather(block, "vocab", axis=1, tiled=True)
    me = lax.axis_index("vocab")
    rows, width = block.shape
    held = block[:, None, :]
    bit = n // 2
    while bit >= 1:
        got = lax.ppermute(held, "vocab", [(k, k ^ bit) for k in range(n)])
        clear = (me // bit) % 2 == 0
        low = jnp.where(clear, held, got)
        high = jnp.where(clear, got, held)
        held = jnp.stack([low, high], axis=2).reshape(rows, 2 * held.shape[1], width)
        bit //= 2
    return held.reshape(rows, n * width)


def doubling_gather(piece):
    n = lax.axis_size("dp")
    if n & (n - 1):
        return lax.all_gather(piece, "dp")
    me = lax.axis_index("dp")
    held = piece[None]
    bit = 1
    while bit < n:
        got = lax.ppermute(held, "dp", [(k, k ^ bit) for k in range(n)])
        low = (me // bit) % 2 == 0
        held = jnp.where(low, jnp.concatenate([held, got]), jnp.concatenate([got, held]))
        bit *= 2
    return held


def shift_exchange(wide, axis):
    n = lax.axis_size("dp")
    me = lax.axis_index("dp")
    own = lax.dynamic_index_in_dim(wide, me, axis, keepdims=True)
    pieces = [own]
    for shift in range(1, n):
        send = lax.dynamic_index_in_dim(wide, (me + shift) % n, axis, keepdims=True)
        pieces.append(lax.ppermute(send, "dp", [(k, (k + shift) % n) for k in range(n)]))
    held = jnp.concatenate(pieces, axis=axis)
    return jnp.take(held, (me - jnp.arange(n)) % n, axis=axis, mode="clip")


def shards(hidden, weight, teacher_ids, teacher_logp, union_blocks):
    tokens_here = hidden.shape[0]
    n_groups = lax.axis_size("dp")
    per_dev = weight.shape[0] // BLOCK
    piece = weight.shape[1]
    width = SLOTS * BLOCK
    dp_row = lax.axis_index("dp")
    column = lax.axis_index("vocab")
    table = slot_table(union_blocks, column, per_dev)
    filled = table >= 0
    local = jnp.where(filled, table - column * per_dev, -1)
    blocks = weight.reshape(per_dev, BLOCK, piece)
    chosen = jnp.take(blocks, jnp.maximum(local, 0).reshape(-1), axis=0, mode="clip").reshape(
        n_groups, width, piece
    )
    full_rows = doubling_rows(hidden)
    wide = full_rows.reshape(tokens_here, n_groups, piece)
    n_vocab = lax.axis_size("vocab")
    pair = n_groups == 2 and n_vocab % 2 == 0 and not n_vocab & (n_vocab - 1)
    if pair:
        first = dp_row == 0
        own_half = jnp.where(first, wide[:, 0], wide[:, 1])
        other_half = jnp.where(first, wide[:, 1], wide[:, 0])
        got_half = lax.ppermute(other_half, "dp", [(0, 1), (1, 0)])
    else:
        halves = shift_exchange(wide, 1)
    own_slots = lax.dynamic_index_in_dim(table, dp_row, 0, keepdims=False)
    col_mask = jnp.repeat(own_slots >= 0, BLOCK)
    if pair:
        slot_rows = jnp.maximum(local, 0)

        def rows_of(tile):
            picks = lax.dynamic_index_in_dim(slot_rows, tile, 0, keepdims=False)
            return jnp.take(blocks, picks, axis=0, mode="clip").reshape(width, piece)

        got_w = lax.ppermute(rows_of(1 - dp_row), "dp", [(0, 1), (1, 0)])
        own_w = rows_of(dp_row)
    else:
        rows_w = shift_exchange(chosen, 0)
    if pair:
        logits = jnp.einsum(
            "td,rd->tr", own_half, own_w, preferred_element_type=jnp.float32
        ) + jnp.einsum("td,rd->tr", other_half, got_w, preferred_element_type=jnp.float32)
    else:
        logits = jnp.einsum("tkd,krd->tr", wide, rows_w, preferred_element_type=jnp.float32)
    offsets = teacher_ids % BLOCK
    match = (teacher_ids // BLOCK)[:, :, None] == own_slots[None, None, :]
    starts = jnp.arange(SLOTS, dtype=jnp.int32) * BLOCK
    position = jnp.sum(jnp.where(match, starts[None, None, :] + offsets[:, :, None], 0), axis=-1)
    hit = jnp.any(match, axis=-1)
    teacher_q = jax.nn.softmax(teacher_logp, axis=-1) * hit.astype(jnp.float32)
    onehot = (position[:, :, None] == jnp.arange(width, dtype=jnp.int32)[None, None, :]).astype(
        jnp.float32
    )
    target = jnp.einsum("tk,tkr->tr", teacher_q, onehot)
    masked = jnp.where(col_mask[None, :], logits, negative)
    local_top = jnp.max(masked, axis=1)
    aimed = jnp.sum(target * logits, axis=1)
    local_total = jnp.sum(jnp.where(col_mask[None, :], jnp.exp(masked - local_top[:, None]), 0.0), axis=1)
    top, total, picked = combine_stats(local_top, local_total, aimed)
    lse = top + jnp.log(total)
    loss = lse - picked
    probs = jnp.where(col_mask[None, :], jnp.exp(logits - lse[:, None]), 0.0)
    dlog = (probs - target).astype(jnp.bfloat16)
    if pair:
        hidden_terms = jnp.stack(
            [
                jnp.einsum("tr,rd->td", dlog, own_w, preferred_element_type=jnp.float32),
                jnp.einsum("tr,rd->td", dlog, got_w, preferred_element_type=jnp.float32),
            ],
            axis=1,
        )
        flip = dp_row * (lax.axis_size("vocab") // 2)
    else:
        hidden_terms = jnp.einsum("tr,krd->tkd", dlog, rows_w, preferred_element_type=jnp.float32)
        flip = 0
    hidden_terms = hidden_terms.reshape(tokens_here, n_groups * piece)
    grad_hidden = halving_scatter(hidden_terms, flip).astype(jnp.bfloat16)
    dlog_all = doubling_gather(dlog).reshape(n_groups, tokens_here, SLOTS, BLOCK)
    block_ids = jnp.arange(per_dev, dtype=jnp.int32)
    placed = jnp.zeros((n_groups, tokens_here, per_dev, BLOCK), jnp.bfloat16)
    for q in range(SLOTS):
        hit_q = local[:, q][:, None] == block_ids[None, :]
        placed = placed + jnp.where(
            hit_q[:, None, :, None], dlog_all[:, :, q, :][:, :, None, :], jnp.zeros((), jnp.bfloat16)
        )
    placed = placed.reshape(n_groups, tokens_here, per_dev * BLOCK)
    grad_weight = weight_grad(pair, placed, dp_row, halves if not pair else None,
                              (own_half, got_half) if pair else None)
    return (loss, grad_hidden, grad_weight)


def weight_grad(pair, placed, dp_row, halves, pieces):
    if pair:
        own_half, got_half = pieces
        mine_p = jnp.where(dp_row == 0, placed[0], placed[1])
        other_p = jnp.where(dp_row == 0, placed[1], placed[0])
        grad_weight = jnp.einsum(
            "tr,td->rd",
            jnp.concatenate([mine_p, other_p]),
            jnp.concatenate([own_half, got_half]),
            preferred_element_type=jnp.float32,
        ).astype(jnp.bfloat16)
    else:
        grad_weight = jnp.einsum(
            "str,tsd->rd", placed, halves, preferred_element_type=jnp.float32
        ).astype(jnp.bfloat16)
    return grad_weight


def solution(mesh):
    return jax.shard_map(
        shards,
        mesh=mesh,
        in_specs=(P("dp", "vocab"), P("vocab", "dp"), P("dp", None), P("dp", None), P()),
        out_specs=(P("dp"), P("dp", "vocab"), P("vocab", "dp")),
        check_vma=False,
    )
```
